128 devices in a mesh: seg: 32 (over y, x, core), head: 4 (over z).
Axes of the slice: x: 4, y: 4, z: 4, core: 2. Of those that a mesh axis runs over, the one named last changes fastest.
Arguments:
- tokens: float32 [16384, 2048], P(('seg', 'head'))
- document_index: int32 [16384], P('seg'), may hold values from 0 to 127, never falling along the last dimension, each value on 1 to 256 neighbouring positions
- block_mask: int32 [32, 4, 4], P('seg'), may hold values from 0 to 1, as said below
- slot_keys: bfloat16 [2, 128, 2048], P(None, None, 'head'), may hold values from -8 to 8
- mem_init: float32 [2, 128, 2048], P(None, None, 'head'), may hold values from -6 to 6
- retain: float32 [2, 32, 32], P(None, 'seg', 'head'), may hold values from 0.005 to 1
- attn_gain: float32 [2, 2048], replicated, may hold values from 0.25 to 4
- mlp_gain: float32 [2, 2048], replicated, may hold values from 0.25 to 4
- w_query: bfloat16 [2, 2048, 2048], P(None, None, 'head')
- w_kv: bfloat16 [2, 2048, 1024], P(None, None, 'head')
- w_out: bfloat16 [2, 2048, 2048], P(None, 'head'), may hold values from -0.125 to 0.125
- w_gate_up: bfloat16 [2, 2048, 2, 4096], P(None, None, None, 'head'), may hold values from -0.125 to 0.125
- w_down: bfloat16 [2, 4096, 2048], P(None, 'head'), may hold values from -0.09375 to 0.09375
Outputs:
- hidden: float32 [16384, 2048], P(('seg', 'head'))
- memory: float32 [2, 32, 128, 2048], P(None, 'seg', None, 'head')
The draws below stay inside these ranges and needn't reach their ends.
Inputs may be any that keep to these rules, and one draw needn't show every extreme that they name: `document_index`: document numbers never fall along the sequence. `block_mask`: in every segment the blocks on the diagonal are 1 and the blocks above it 0.
All inputs are finite; a program needn't handle non-finite values.
Results may differ from the reference program's by a relative error of at most 0.025.
Values may be sent and summed in bfloat16 or wider, within the bound.
No kernel may reach another device: no remote copies, remote signals or barrier semaphores. Data moves between devices by JAX's collectives and lax.ppermute only.
A program may use at most 192 MiB of HBM per device.

```python
import math
import jax
import jax.numpy as jnp
import numpy as np
from jax import lax

D = 2048
HEADS = 32
KV_HEADS = 8
HD = 64
FF = 4096
MEM = 128
SEG_LEN = 512
BLOCK = 128
DEPTH_NUMBER = 2
PIECE_NUMBER = 32
SEQ = 16384


def draw_tokens(key, part):
    first_key = jax.random.fold_in(key, 0)
    return jax.random.normal(first_key, (SEQ, D), jnp.float32)


def draw_block_mask(key, part):
    count = SEG_LEN // BLOCK
    bits = jax.random.randint(key, (PIECE_NUMBER, count, count), 0, 2)
    row_at = jnp.arange(count)[:, None]
    col_at = jnp.arange(count)[None, :]
    return jnp.where(row_at == col_at, 1, jnp.where(row_at > col_at, bits, 0)).astype(jnp.int32)


def draw_slot_keys(key, part):
    base = jax.random.fold_in(key, 29)
    entry_key = jax.random.fold_in(base, 0)
    entries = jax.random.normal(entry_key, (DEPTH_NUMBER, MEM, HEADS * HD), jnp.float32)
    return jnp.clip(entries, -4.0, 4.0).astype(jnp.bfloat16)


def draw_retain(key, part):
    lookup_vectors = jax.random.split(key, 5)
    share = 0.5
    pick = jax.random.uniform(lookup_vectors[0], (DEPTH_NUMBER, 1, HEADS), jnp.float32)
    fast = jax.random.uniform(lookup_vectors[1], (DEPTH_NUMBER, PIECE_NUMBER, HEADS), jnp.float32, 0.03, 0.3)
    gradual_memory = jnp.exp(jnp.log(0.1) * jax.random.uniform(lookup_vectors[2], (DEPTH_NUMBER, PIECE_NUMBER, HEADS), jnp.float32, 0.1, 0.6) / PIECE_NUMBER)
    symbol_group = jax.random.uniform(lookup_vectors[3], (DEPTH_NUMBER, PIECE_NUMBER, 1), jnp.float32) < 2.5 / PIECE_NUMBER
    split_location = jax.random.uniform(lookup_vectors[4], (DEPTH_NUMBER, PIECE_NUMBER, HEADS), jnp.float32, 0.5, 0.8)
    gradual_memory = jnp.where(symbol_group, gradual_memory * split_location, gradual_memory)
    return jnp.where(pick < share, fast, gradual_memory).astype(jnp.float32)


def projections(key):
    base = jax.random.fold_in(key, 17)
    query_key, pair_key = jax.random.split(base, 2)
    factor = D ** (-0.5)
    pair_weight = jax.random.normal(pair_key, (DEPTH_NUMBER, D, KV_HEADS * 2 * HD), jnp.float32) * factor
    query_weight = jax.random.normal(query_key, (DEPTH_NUMBER, D, HEADS * HD), jnp.float32) * factor
    return (query_weight, pair_weight)


def draw_w_query(key, part):
    return projections(key)[0].astype(jnp.bfloat16)


def draw_w_kv(key, part):
    return projections(key)[1].astype(jnp.bfloat16)


def levels(rng, dims, cuts, smallest, top_value):
    loudness = 1.0
    for dim, blocks in cuts:
        draws = jax.random.uniform(jax.random.fold_in(jax.random.fold_in(rng, 6), dim), (blocks,), jnp.float32, smallest / len(cuts), top_value / len(cuts))
        loudness = loudness * jnp.repeat(jnp.exp(draws), dims[dim] // blocks).reshape((-1,) + (1,) * (len(dims) - 1 - dim))
    return loudness


def length_profile(count, total, bound, skew):
    loads = [(1 << 20) // math.isqrt(rank ** skew) + 1 for rank in range(2, count + 1)]
    surplus, counts = total - bound - (count - 1), [1] * (count - 1)
    while surplus > 0:
        free = [i for i in range(count - 1) if counts[i] < bound]
        whole, left = sum([loads[i] for i in free]), surplus
        for i in free:
            addition = min(bound - counts[i], max(1, left * loads[i] // whole), surplus)
            counts[i] = counts[i] + addition
            surplus = surplus - addition
    return np.array([bound] + counts)


def ragged(own_key, number_of, total, most, skew):
    if number_of == 2:
        one = jax.random.randint(own_key, (), max(1, total - most), min(most, total - 1) + 1)
        return jnp.stack([one, total - one])
    lengths = jnp.asarray(length_profile(number_of, total, most, skew), jnp.int32)
    twos = (number_of - 1) // 2
    giver, sink = lengths[1:1 + 2 * twos:2], lengths[2:2 + 2 * twos:2]
    room = jnp.minimum(giver - 1, most - sink)
    passed = jax.random.randint(jax.random.fold_in(own_key, 1), (twos,), 0, 1 << 20) % (room + 1)
    lengths = lengths.at[1:1 + 2 * twos:2].set(giver - passed).at[2:2 + 2 * twos:2].set(sink + passed)
    return lengths[jax.random.permutation(jax.random.fold_in(own_key, 2), number_of)]


def centred(own_key, dims, spread, limit, cuts=(), held_as=jnp.bfloat16):
    values = spread * jax.random.normal(own_key, dims, jnp.float32)
    if cuts:
        values = values * levels(own_key, dims, cuts, -0.22, 0.18)
    return jnp.clip(values, -limit, limit).astype(held_as)


def setup_inputs(seed: int = 0) -> dict:
    keys = jax.random.split(jax.random.key(seed), 14)
    tokens = draw_tokens(jax.random.fold_in(keys[13], 71), 0)
    document_index = jnp.searchsorted(jnp.cumsum(ragged(keys[1], 4 * PIECE_NUMBER, SEQ, SEG_LEN // 2, 2)), jnp.arange(SEQ), side="right").astype(jnp.int32)
    block_mask = draw_block_mask(jax.random.fold_in(keys[13], 71), 0)
    slot_keys = draw_slot_keys(jax.random.fold_in(keys[13], 71), 0)
    mem_init = centred(keys[4], (DEPTH_NUMBER, MEM, HEADS * HD), 1.0, 6.0, ((2, 4),), jnp.float32)
    retain = draw_retain(jax.random.fold_in(keys[13], 71), 0)
    attn_gain = jnp.clip(jnp.exp(jax.random.uniform(keys[6], (DEPTH_NUMBER, D), jnp.float32, math.log(0.25), math.log(4.0))), 0.25, 4.0)
    mlp_gain = jnp.clip(jnp.exp(jax.random.uniform(keys[7], (DEPTH_NUMBER, D), jnp.float32, math.log(0.25), math.log(4.0))), 0.25, 4.0)
    w_query = draw_w_query(jax.random.fold_in(keys[13], 71), 0)
    w_kv = draw_w_kv(jax.random.fold_in(keys[13], 71), 0)
    w_out = centred(keys[10], (DEPTH_NUMBER, HEADS * HD, D), (HEADS * HD) ** -0.5, 0.125, ((1, 4),))
    w_gate_up = centred(keys[11], (DEPTH_NUMBER, D, 2, FF), D ** -0.5, 0.125, ((3, 4),))
    w_down = centred(keys[12], (DEPTH_NUMBER, FF, D), FF ** -0.5, 0.09375, ((1, 4),))
    return dict(tokens=tokens, document_index=document_index, block_mask=block_mask, slot_keys=slot_keys, mem_init=mem_init, retain=retain, attn_gain=attn_gain, mlp_gain=mlp_gain, w_query=w_query, w_kv=w_kv, w_out=w_out, w_gate_up=w_gate_up, w_down=w_down)


def rounded(value):
    return lax.optimization_barrier(value.astype(jnp.bfloat16)).astype(jnp.float32)

def rms_norm(value, gain):
    wide = value.astype(jnp.float32)
    factor = lax.rsqrt(lax.optimization_barrier(jnp.mean(wide * wide, axis=-1, keepdims=True)) + 1e-05)
    return (wide * factor * gain).astype(jnp.bfloat16)

def rope_tables(position):
    half = HD // 2
    freq = 500000.0 ** (-(jnp.arange(half).astype(jnp.float32) * 2.0 / HD))
    angle = position.astype(jnp.float32)[:, None] * freq[None, :]
    return (jnp.cos(angle), jnp.sin(angle))

def rotate(tensor, cosine, sine):
    half = tensor.shape[-1] // 2
    first = tensor[..., :half]
    second = tensor[..., half:]
    cos_part = cosine[:, None, :]
    sin_part = sine[:, None, :]
    return jnp.concatenate([first * cos_part - second * sin_part, second * cos_part + first * sin_part], axis=-1)

def reference(tokens, document_index, block_mask, slot_keys, mem_init, retain, attn_gain, mlp_gain, w_query, w_kv, w_out, w_gate_up, w_down):
    group = HEADS // KV_HEADS
    scale = HD ** (-0.5)
    cosine, sine = rope_tables(jnp.arange(SEQ) % SEG_LEN)
    docs = document_index.reshape(PIECE_NUMBER, SEG_LEN)
    causal = jnp.arange(SEG_LEN)[:, None] >= jnp.arange(SEG_LEN)[None, :]
    stream = tokens
    stored = []
    for layer in range(DEPTH_NUMBER):
        normed = rms_norm(stream, attn_gain[layer])
        query = jnp.dot(normed, w_query[layer], preferred_element_type=jnp.float32)
        pairs = jnp.dot(normed, w_kv[layer], preferred_element_type=jnp.float32).reshape(SEQ, KV_HEADS, 2, HD)
        query = rotate(query.reshape(SEQ, HEADS, HD), cosine, sine).astype(jnp.bfloat16).reshape(PIECE_NUMBER, SEG_LEN, KV_HEADS, group, HD)
        lookup_vectors = rotate(pairs[:, :, 0], cosine, sine).astype(jnp.bfloat16).reshape(PIECE_NUMBER, SEG_LEN, KV_HEADS, HD)
        values = pairs[:, :, 1].astype(jnp.bfloat16).reshape(PIECE_NUMBER, SEG_LEN, KV_HEADS, HD)
        slots = slot_keys[layer].reshape(MEM, KV_HEADS, group, HD).astype(jnp.float32)

        def write_one(inputs):
            seg_keys, seg_values = inputs
            scores = jnp.einsum('mkgd,jkd->kgmj', slots, seg_keys.astype(jnp.float32)) * scale
            probs = rounded(jax.nn.softmax(scores, axis=-1))
            return jnp.einsum('kgmj,jkd->mkgd', probs, seg_values.astype(jnp.float32)).reshape(MEM, HEADS * HD)
        written = lax.map(write_one, (lookup_vectors, values))
        rates = jnp.repeat(retain[layer], HD, axis=1)[:, None, :]

        def advance(state, inputs):
            rate, fresh = inputs
            after = rate * state + (1.0 - rate) * fresh
            return (after, (state, after))
        final_state, (before, after) = lax.scan(advance, mem_init[layer], (rates, written))
        stored.append(after)

        def fetch_single(inputs):
            seg_query, seg_keys, seg_values, memory_state, seg_docs, seg_blocks = inputs
            blocks = jnp.repeat(jnp.repeat(seg_blocks, BLOCK, axis=0), BLOCK, axis=1)
            allowed = causal & (seg_docs[:, None] == seg_docs[None, :]) & (blocks == 1)
            query_wide = seg_query.astype(jnp.float32)
            slot_scores = jnp.einsum('ikgd,mkgd->kgim', query_wide, slots) * scale
            token_scores = jnp.einsum('ikgd,jkd->kgij', query_wide, seg_keys.astype(jnp.float32)) * scale
            token_scores = jnp.where(allowed, token_scores, -jnp.inf)
            probs = rounded(jax.nn.softmax(jnp.concatenate([slot_scores, token_scores], axis=-1), axis=-1))
            memory_read = rounded(memory_state).reshape(MEM, KV_HEADS, group, HD)
            result = jnp.einsum('kgim,mkgd->ikgd', probs[..., :MEM], memory_read)
            result = result + jnp.einsum('kgij,jkd->ikgd', probs[..., MEM:], seg_values.astype(jnp.float32))
            return result.reshape(SEG_LEN, HEADS * HD).astype(jnp.bfloat16)
        attended = lax.map(fetch_single, (query, lookup_vectors, values, before, docs, block_mask)).reshape(SEQ, HEADS * HD)
        mixed = jnp.dot(attended, w_out[layer], preferred_element_type=jnp.float32)
        middle = stream + mixed
        normed = rms_norm(middle, mlp_gain[layer])
        gate = jnp.dot(normed, w_gate_up[layer][:, 0], preferred_element_type=jnp.float32)
        upper = jnp.dot(normed, w_gate_up[layer][:, 1], preferred_element_type=jnp.float32)
        inner = (jax.nn.silu(gate) * upper).astype(jnp.bfloat16)
        down = jnp.dot(inner, w_down[layer], preferred_element_type=jnp.float32)
        stream = middle + down
    return (stream, jnp.stack(stored))
```

```python
import jax
import jax.numpy as jnp
from jax import lax
from jax.sharding import PartitionSpec as P

HEADS = 32
KV_HEADS = 8
HD = 64
MEM = 128
SEG_LEN = 512
BLOCK = 128
DEPTH_NUMBER = 2


def rms_norm(value, gain):
    factor = lax.rsqrt(jnp.mean(value * value, axis=-1, keepdims=True) + 1e-05)
    return (value * factor * gain).astype(jnp.bfloat16)


def rope_tables(position):
    half = HD // 2
    freq = 500000.0 ** (-(jnp.arange(half).astype(jnp.float32) * 2.0 / HD))
    angle = position.astype(jnp.float32)[:, None] * freq[None, :]
    return (jnp.cos(angle), jnp.sin(angle))


def rotate(tensor, cosine, sine):
    half = tensor.shape[-1] // 2
    first = tensor[..., :half]
    second = tensor[..., half:]
    cos_part = cosine[:, None, :]
    sin_part = sine[:, None, :]
    return jnp.concatenate(
        [first * cos_part - second * sin_part, second * cos_part + first * sin_part], axis=-1
    )


def body(
    tokens,
    document_index,
    block_mask,
    slot_keys,
    mem_init,
    retain,
    attn_gain,
    mlp_gain,
    w_query,
    w_kv,
    w_out,
    w_gate_up,
    w_down,
):
    seg_local = document_index.shape[0] // SEG_LEN
    rows_all = seg_local * SEG_LEN
    cols_query = w_query.shape[2]
    local_heads = cols_query // HD
    group = HEADS // KV_HEADS
    local_kv = local_heads // group
    scale = HD ** (-0.5)
    cosine, sine = rope_tables(jnp.arange(rows_all) % SEG_LEN)
    docs = document_index.reshape(seg_local, SEG_LEN)
    causal = jnp.arange(SEG_LEN)[:, None] >= jnp.arange(SEG_LEN)[None, :]
    stream = tokens
    stored = []
    for layer in range(DEPTH_NUMBER):
        query_weight = w_query[layer]
        pair_weight = w_kv[layer]
        out_weight = w_out[layer]
        widening_matrix = w_gate_up[layer]
        down_weight = w_down[layer]
        normed = rms_norm(stream, attn_gain[layer])
        project_piece = lax.all_gather(normed, "head", axis=0, tiled=True)
        projected = jnp.concatenate(
            [
                jnp.dot(project_piece, query_weight, preferred_element_type=jnp.float32),
                jnp.dot(project_piece, pair_weight, preferred_element_type=jnp.float32),
            ],
            axis=1,
        )
        query = rotate(
            projected[:, :cols_query].reshape(rows_all, local_heads, HD), cosine, sine
        ).astype(jnp.bfloat16)
        pairs = projected[:, cols_query:].reshape(rows_all, local_kv, 2, HD)
        lookup_vectors = rotate(pairs[:, :, 0], cosine, sine).astype(jnp.bfloat16)
        values = pairs[:, :, 1].astype(jnp.bfloat16)
        query = query.reshape(seg_local, SEG_LEN, local_kv, group, HD)
        lookup_vectors = lookup_vectors.reshape(seg_local, SEG_LEN, local_kv, HD)
        values = values.reshape(seg_local, SEG_LEN, local_kv, HD)
        slots = slot_keys[layer].reshape(MEM, local_kv, group, HD)
        write_scores = (
            jnp.einsum(
                "mkgd,sjkd->skgmj", slots, lookup_vectors, preferred_element_type=jnp.float32
            )
            * scale
        )
        write_probs = jax.nn.softmax(write_scores, axis=-1).astype(jnp.bfloat16)
        written = jnp.einsum(
            "skgmj,sjkd->smkgd", write_probs, values, preferred_element_type=jnp.float32
        ).reshape(seg_local, MEM, cols_query)
        rates = jnp.repeat(retain[layer], HD, axis=1)[:, None, :]
        here = lax.axis_index("seg")
        count = lax.axis_size("seg")
        rate_all = lax.all_gather(retain[layer][0], "seg")
        written_all = lax.all_gather(written[0], "seg")
        order = jnp.arange(count)
        inside = (order[None, :] > order[:, None]) & (order[None, :] < here)
        span = jnp.prod(jnp.where(inside[:, :, None], rate_all[None, :, :], 1.0), axis=1)
        weight = jnp.where((order < here)[:, None], span * (1.0 - rate_all), 0.0)
        carry = jnp.prod(jnp.where((order < here)[:, None], rate_all, 1.0), axis=0)
        weight = jnp.repeat(weight, HD, axis=1)
        carry = jnp.repeat(carry, HD)
        state = carry[None, :] * mem_init[layer] + jnp.sum(
            weight[:, None, :] * written_all, axis=0
        )
        segment = 0
        memory_read = state.astype(jnp.bfloat16).reshape(MEM, local_kv, group, HD)
        state = rates[segment] * state + (1.0 - rates[segment]) * written[segment]
        after_list = [state]
        blocks = jnp.repeat(jnp.repeat(block_mask[segment], BLOCK, axis=0), BLOCK, axis=1)
        allowed = causal & (docs[segment][:, None] == docs[segment][None, :]) & (blocks == 1)
        slot_scores = (
            jnp.einsum("ikgd,mkgd->kgim", query[segment], slots, preferred_element_type=jnp.float32)
            * scale
        )
        token_scores = (
            jnp.einsum(
                "ikgd,jkd->kgij",
                query[segment],
                lookup_vectors[segment],
                preferred_element_type=jnp.float32,
            )
            * scale
        )
        token_scores = jnp.where(allowed, token_scores, -jnp.inf)
        probs = jax.nn.softmax(
            jnp.concatenate([slot_scores, token_scores], axis=-1), axis=-1
        ).astype(jnp.bfloat16)
        result = jnp.einsum(
            "kgim,mkgd->ikgd", probs[..., :MEM], memory_read, preferred_element_type=jnp.float32
        )
        result = result + jnp.einsum(
            "kgij,jkd->ikgd", probs[..., MEM:], values[segment], preferred_element_type=jnp.float32
        )
        outputs = result.reshape(SEG_LEN, cols_query).astype(jnp.bfloat16)
        stored.append(jnp.stack(after_list))
        mixed = lax.psum_scatter(
            jnp.dot(outputs, out_weight, preferred_element_type=jnp.float32).astype(jnp.bfloat16),
            "head",
            scatter_dimension=0,
            tiled=True,
        )
        middle = stream + mixed.astype(jnp.float32)
        both = jnp.einsum(
            "rd,dtf->rtf",
            lax.all_gather(rms_norm(middle, mlp_gain[layer]), "head", axis=0, tiled=True),
            widening_matrix,
            preferred_element_type=jnp.float32,
        )
        inner = (jax.nn.silu(both[:, 0]) * both[:, 1]).astype(jnp.bfloat16)
        down = lax.psum_scatter(
            jnp.dot(inner, down_weight, preferred_element_type=jnp.float32).astype(jnp.bfloat16),
            "head",
            scatter_dimension=0,
            tiled=True,
        )
        stream = middle + down.astype(jnp.float32)
    return (stream, jnp.stack(stored))


def solution(mesh):
    return jax.shard_map(
        body,
        mesh=mesh,
        in_specs=(
            P(("seg", "head"), None),
            P("seg"),
            P("seg", None, None),
            P(None, None, "head"),
            P(None, None, "head"),
            P(None, "seg", "head"),
            P(),
            P(),
            P(None, None, "head"),
            P(None, None, "head"),
            P(None, "head", None),
            P(None, None, None, "head"),
            P(None, "head", None),
        ),
        out_specs=(P(("seg", "head"), None), P(None, "seg", None, "head")),
        check_vma=False,
    )
```

```python
import jax
import jax.numpy as jnp
from jax import lax
from jax.sharding import PartitionSpec as P

HEADS = 32
KV_HEADS = 8
HD = 64
MEM = 128
SEG_LEN = 512
BLOCK = 128
DEPTH_NUMBER = 2


def rms_norm(value, gain):
    factor = lax.rsqrt(jnp.mean(value * value, axis=-1, keepdims=True) + 1e-05)
    return (value * factor * gain).astype(jnp.bfloat16)


def rope_tables(position):
    half = HD // 2
    freq = 500000.0 ** (-(jnp.arange(half).astype(jnp.float32) * 2.0 / HD))
    angle = position.astype(jnp.float32)[:, None] * freq[None, :]
    return (jnp.cos(angle), jnp.sin(angle))


def rotate(tensor, cosine, sine):
    half = tensor.shape[-1] // 2
    first = tensor[..., :half]
    second = tensor[..., half:]
    cos_part = cosine[:, None, :]
    sin_part = sine[:, None, :]
    return jnp.concatenate(
        [first * cos_part - second * sin_part, second * cos_part + first * sin_part], axis=-1
    )


def body(
    tokens,
    document_index,
    block_mask,
    slot_keys,
    mem_init,
    retain,
    attn_gain,
    mlp_gain,
    w_query,
    w_kv,
    w_out,
    w_gate_up,
    w_down,
):
    seg_local = document_index.shape[0] // SEG_LEN
    rows_all = seg_local * SEG_LEN
    cols_query = w_query.shape[2]
    local_heads = cols_query // HD
    group = HEADS // KV_HEADS
    local_kv = local_heads // group
    scale = HD ** (-0.5)
    cosine, sine = rope_tables(jnp.arange(rows_all) % SEG_LEN)
    docs = document_index.reshape(seg_local, SEG_LEN)
    causal = jnp.arange(SEG_LEN)[:, None] >= jnp.arange(SEG_LEN)[None, :]
    stream = tokens
    stored = []
    for layer in range(DEPTH_NUMBER):
        query_weight = w_query[layer]
        pair_weight = w_kv[layer]
        out_weight = w_out[layer]
        widening_matrix = w_gate_up[layer]
        down_weight = w_down[layer]
        normed = rms_norm(stream, attn_gain[layer])
        project_piece = lax.all_gather(normed, "head", axis=0, tiled=True)
        projected = jnp.concatenate(
            [
                jnp.dot(project_piece, query_weight, preferred_element_type=jnp.float32),
                jnp.dot(project_piece, pair_weight, preferred_element_type=jnp.float32),
            ],
            axis=1,
        )
        query = rotate(
            projected[:, :cols_query].reshape(rows_all, local_heads, HD), cosine, sine
        ).astype(jnp.bfloat16)
        pairs = projected[:, cols_query:].reshape(rows_all, local_kv, 2, HD)
        lookup_vectors = rotate(pairs[:, :, 0], cosine, sine).astype(jnp.bfloat16)
        values = pairs[:, :, 1].astype(jnp.bfloat16)
        query = query.reshape(seg_local, SEG_LEN, local_kv, group, HD)
        lookup_vectors = lookup_vectors.reshape(seg_local, SEG_LEN, local_kv, HD)
        values = values.reshape(seg_local, SEG_LEN, local_kv, HD)
        slots = slot_keys[layer].reshape(MEM, local_kv, group, HD)
        write_scores = (
            jnp.einsum(
                "mkgd,sjkd->skgmj", slots, lookup_vectors, preferred_element_type=jnp.float32
            )
            * scale
        )
        write_probs = jax.nn.softmax(write_scores, axis=-1).astype(jnp.bfloat16)
        written = jnp.einsum(
            "skgmj,sjkd->smkgd", write_probs, values, preferred_element_type=jnp.float32
        ).reshape(seg_local, MEM, cols_query)
        rates = jnp.repeat(retain[layer], HD, axis=1)[:, None, :]
        here = lax.axis_index("seg")
        count = lax.axis_size("seg")
        rate_row = rates[0]
        rate_high = rate_row.astype(jnp.bfloat16)
        rest = rate_row - rate_high.astype(jnp.float32)
        rate_mid = rest.astype(jnp.bfloat16)
        rate_low = (rest - rate_mid.astype(jnp.float32)).astype(jnp.bfloat16)
        payload = jnp.concatenate(
            [written[0].astype(jnp.bfloat16), rate_high, rate_mid, rate_low], axis=0
        )
        gathered = lax.all_gather(payload, "seg")
        written_all = gathered[:, :MEM].astype(jnp.float32)
        rate_parts = gathered[:, MEM:, ::HD].astype(jnp.float32)
        rate_all = rate_parts[:, 0] + rate_parts[:, 1] + rate_parts[:, 2]
        order = jnp.arange(count)
        inside = (order[None, :] > order[:, None]) & (order[None, :] < here)
        span = jnp.prod(jnp.where(inside[:, :, None], rate_all[None, :, :], 1.0), axis=1)
        weight = jnp.where((order < here)[:, None], span * (1.0 - rate_all), 0.0)
        carry = jnp.prod(jnp.where((order < here)[:, None], rate_all, 1.0), axis=0)
        weight = jnp.repeat(weight, HD, axis=1)
        carry = jnp.repeat(carry, HD)
        state = carry[None, :] * mem_init[layer] + jnp.sum(
            weight[:, None, :] * written_all, axis=0
        )
        segment = 0
        memory_read = state.astype(jnp.bfloat16).reshape(MEM, local_kv, group, HD)
        state = rates[segment] * state + (1.0 - rates[segment]) * written[segment]
        after_list = [state]
        blocks = jnp.repeat(jnp.repeat(block_mask[segment], BLOCK, axis=0), BLOCK, axis=1)
        allowed = causal & (docs[segment][:, None] == docs[segment][None, :]) & (blocks == 1)
        slot_scores = (
            jnp.einsum("ikgd,mkgd->kgim", query[segment], slots, preferred_element_type=jnp.float32)
            * scale
        )
        token_scores = (
            jnp.einsum(
                "ikgd,jkd->kgij",
                query[segment],
                lookup_vectors[segment],
                preferred_element_type=jnp.float32,
            )
            * scale
        )
        token_scores = jnp.where(allowed, token_scores, -jnp.inf)
        probs = jax.nn.softmax(
            jnp.concatenate([slot_scores, token_scores], axis=-1), axis=-1
        ).astype(jnp.bfloat16)
        result = jnp.einsum(
            "kgim,mkgd->ikgd", probs[..., :MEM], memory_read, preferred_element_type=jnp.float32
        )
        result = result + jnp.einsum(
            "kgij,jkd->ikgd", probs[..., MEM:], values[segment], preferred_element_type=jnp.float32
        )
        outputs = result.reshape(SEG_LEN, cols_query).astype(jnp.bfloat16)
        stored.append(jnp.stack(after_list))
        mixed = lax.psum_scatter(
            jnp.dot(outputs, out_weight, preferred_element_type=jnp.float32).astype(jnp.bfloat16),
            "head",
            scatter_dimension=0,
            tiled=True,
        )
        middle = stream + mixed.astype(jnp.float32)
        both = jnp.einsum(
            "rd,dtf->rtf",
            lax.all_gather(rms_norm(middle, mlp_gain[layer]), "head", axis=0, tiled=True),
            widening_matrix,
            preferred_element_type=jnp.float32,
        )
        inner = (jax.nn.silu(both[:, 0]) * both[:, 1]).astype(jnp.bfloat16)
        down = lax.psum_scatter(
            jnp.dot(inner, down_weight, preferred_element_type=jnp.float32).astype(jnp.bfloat16),
            "head",
            scatter_dimension=0,
            tiled=True,
        )
        stream = middle + down.astype(jnp.float32)
    return (stream, jnp.stack(stored))


def solution(mesh):
    return jax.shard_map(
        body,
        mesh=mesh,
        in_specs=(
            P(("seg", "head"), None),
            P("seg"),
            P("seg", None, None),
            P(None, None, "head"),
            P(None, None, "head"),
            P(None, "seg", "head"),
            P(),
            P(),
            P(None, None, "head"),
            P(None, None, "head"),
            P(None, "head", None),
            P(None, None, None, "head"),
            P(None, "head", None),
        ),
        out_specs=(P(("seg", "head"), None), P(None, "seg", None, "head")),
        check_vma=False,
    )
```

```python
import jax
import jax.numpy as jnp
from jax import lax
from jax.sharding import PartitionSpec as P

HEADS = 32
KV_HEADS = 8
HD = 64
MEM = 128
SEG_LEN = 512
BLOCK = 128
DEPTH_NUMBER = 2


def ring_pairs(count, step):
    return [(i, (i + step) % count) for i in range(count)]


def ring_gather(piece, axis):
    count = lax.axis_size(axis)
    here = lax.axis_index(axis)
    rows = piece.shape[0]
    half = rows // 2
    ahead = ring_pairs(count, 1)
    behind = ring_pairs(count, -1)
    from_before = lax.ppermute(piece, axis, ahead)
    from_after = lax.ppermute(piece, axis, behind)
    far_top = lax.ppermute(from_before[:half], axis, ahead)
    far_bottom = lax.ppermute(from_after[half:], axis, behind)
    relative = jnp.concatenate([piece, from_after, far_top, far_bottom, from_before], axis=0)
    return jnp.roll(relative, here * rows, axis=0)


def ring_scatter(whole, axis):
    count = lax.axis_size(axis)
    here = lax.axis_index(axis)
    rows = whole.shape[0] // count
    half = rows // 2
    ahead = ring_pairs(count, 1)
    behind = ring_pairs(count, -1)

    def block(offset):
        return lax.dynamic_slice_in_dim(whole, ((here + offset) % count) * rows, rows)

    far = block(2)
    sent_top = lax.ppermute(far[:half].astype(jnp.bfloat16), axis, ahead)
    sent_bottom = lax.ppermute(far[half:].astype(jnp.bfloat16), axis, behind)
    next_part = block(1)
    next_part = jnp.concatenate([next_part[:half] + sent_top.astype(jnp.float32), next_part[half:]])
    prev_part = block(-1)
    prev_part = jnp.concatenate([prev_part[:half], prev_part[half:] + sent_bottom.astype(jnp.float32)])
    got_before = lax.ppermute(next_part.astype(jnp.bfloat16), axis, ahead)
    got_after = lax.ppermute(prev_part.astype(jnp.bfloat16), axis, behind)
    return block(0) + got_before.astype(jnp.float32) + got_after.astype(jnp.float32)


def rms_norm(value, gain):
    factor = lax.rsqrt(jnp.mean(value * value, axis=-1, keepdims=True) + 1e-05)
    return (value * factor * gain).astype(jnp.bfloat16)


def rope_tables(position):
    half = HD // 2
    freq = 500000.0 ** (-(jnp.arange(half).astype(jnp.float32) * 2.0 / HD))
    angle = position.astype(jnp.float32)[:, None] * freq[None, :]
    return (jnp.cos(angle), jnp.sin(angle))


def rotate(tensor, cosine, sine):
    half = tensor.shape[-1] // 2
    first = tensor[..., :half]
    second = tensor[..., half:]
    cos_part = cosine[:, None, :]
    sin_part = sine[:, None, :]
    return jnp.concatenate(
        [first * cos_part - second * sin_part, second * cos_part + first * sin_part], axis=-1
    )


def body(
    tokens,
    document_index,
    block_mask,
    slot_keys,
    mem_init,
    retain,
    attn_gain,
    mlp_gain,
    w_query,
    w_kv,
    w_out,
    w_gate_up,
    w_down,
):
    seg_local = document_index.shape[0] // SEG_LEN
    rows_all = seg_local * SEG_LEN
    cols_query = w_query.shape[2]
    local_heads = cols_query // HD
    group = HEADS // KV_HEADS
    local_kv = local_heads // group
    scale = HD ** (-0.5)
    cosine, sine = rope_tables(jnp.arange(rows_all) % SEG_LEN)
    docs = document_index.reshape(seg_local, SEG_LEN)
    causal = jnp.arange(SEG_LEN)[:, None] >= jnp.arange(SEG_LEN)[None, :]
    stream = tokens
    stored = []
    for layer in range(DEPTH_NUMBER):
        query_weight = w_query[layer]
        pair_weight = w_kv[layer]
        out_weight = w_out[layer]
        widening_matrix = w_gate_up[layer]
        down_weight = w_down[layer]
        normed = rms_norm(stream, attn_gain[layer])
        project_piece = ring_gather(normed, "head")
        projected = jnp.concatenate(
            [
                jnp.dot(project_piece, query_weight, preferred_element_type=jnp.float32),
                jnp.dot(project_piece, pair_weight, preferred_element_type=jnp.float32),
            ],
            axis=1,
        )
        query = rotate(
            projected[:, :cols_query].reshape(rows_all, local_heads, HD), cosine, sine
        ).astype(jnp.bfloat16)
        pairs = projected[:, cols_query:].reshape(rows_all, local_kv, 2, HD)
        lookup_vectors = rotate(pairs[:, :, 0], cosine, sine).astype(jnp.bfloat16)
        values = pairs[:, :, 1].astype(jnp.bfloat16)
        query = query.reshape(seg_local, SEG_LEN, local_kv, group, HD)
        lookup_vectors = lookup_vectors.reshape(seg_local, SEG_LEN, local_kv, HD)
        values = values.reshape(seg_local, SEG_LEN, local_kv, HD)
        slots = slot_keys[layer].reshape(MEM, local_kv, group, HD)
        write_scores = (
            jnp.einsum(
                "mkgd,sjkd->skgmj", slots, lookup_vectors, preferred_element_type=jnp.float32
            )
            * scale
        )
        write_probs = jax.nn.softmax(write_scores, axis=-1).astype(jnp.bfloat16)
        written = jnp.einsum(
            "skgmj,sjkd->smkgd", write_probs, values, preferred_element_type=jnp.float32
        ).reshape(seg_local, MEM, cols_query)
        rates = jnp.repeat(retain[layer], HD, axis=1)[:, None, :]
        here = lax.axis_index("seg")
        count = lax.axis_size("seg")
        rate_row = rates[0]
        rate_high = rate_row.astype(jnp.bfloat16)
        rest = rate_row - rate_high.astype(jnp.float32)
        rate_mid = rest.astype(jnp.bfloat16)
        rate_low = (rest - rate_mid.astype(jnp.float32)).astype(jnp.bfloat16)
        payload = jnp.concatenate(
            [written[0].astype(jnp.bfloat16), rate_high, rate_mid, rate_low], axis=0
        )
        gathered = lax.all_gather(payload, "seg")
        written_all = gathered[:, :MEM].astype(jnp.float32)
        rate_parts = gathered[:, MEM:, ::HD].astype(jnp.float32)
        rate_all = rate_parts[:, 0] + rate_parts[:, 1] + rate_parts[:, 2]
        order = jnp.arange(count)
        inside = (order[None, :] > order[:, None]) & (order[None, :] < here)
        span = jnp.prod(jnp.where(inside[:, :, None], rate_all[None, :, :], 1.0), axis=1)
        weight = jnp.where((order < here)[:, None], span * (1.0 - rate_all), 0.0)
        carry = jnp.prod(jnp.where((order < here)[:, None], rate_all, 1.0), axis=0)
        weight = jnp.repeat(weight, HD, axis=1)
        carry = jnp.repeat(carry, HD)
        state = carry[None, :] * mem_init[layer] + jnp.sum(
            weight[:, None, :] * written_all, axis=0
        )
        segment = 0
        memory_read = state.astype(jnp.bfloat16).reshape(MEM, local_kv, group, HD)
        state = rates[segment] * state + (1.0 - rates[segment]) * written[segment]
        after_list = [state]
        blocks = jnp.repeat(jnp.repeat(block_mask[segment], BLOCK, axis=0), BLOCK, axis=1)
        allowed = causal & (docs[segment][:, None] == docs[segment][None, :]) & (blocks == 1)
        slot_scores = (
            jnp.einsum("ikgd,mkgd->kgim", query[segment], slots, preferred_element_type=jnp.float32)
            * scale
        )
        token_scores = (
            jnp.einsum(
                "ikgd,jkd->kgij",
                query[segment],
                lookup_vectors[segment],
                preferred_element_type=jnp.float32,
            )
            * scale
        )
        token_scores = jnp.where(allowed, token_scores, -jnp.inf)
        probs = jax.nn.softmax(
            jnp.concatenate([slot_scores, token_scores], axis=-1), axis=-1
        ).astype(jnp.bfloat16)
        result = jnp.einsum(
            "kgim,mkgd->ikgd", probs[..., :MEM], memory_read, preferred_element_type=jnp.float32
        )
        result = result + jnp.einsum(
            "kgij,jkd->ikgd", probs[..., MEM:], values[segment], preferred_element_type=jnp.float32
        )
        outputs = result.reshape(SEG_LEN, cols_query).astype(jnp.bfloat16)
        stored.append(jnp.stack(after_list))
        mixed = ring_scatter(
            jnp.dot(outputs, out_weight, preferred_element_type=jnp.float32), "head"
        )
        middle = stream + mixed
        both = jnp.einsum(
            "rd,dtf->rtf",
            ring_gather(rms_norm(middle, mlp_gain[layer]), "head"),
            widening_matrix,
            preferred_element_type=jnp.float32,
        )
        inner = (jax.nn.silu(both[:, 0]) * both[:, 1]).astype(jnp.bfloat16)
        down = ring_scatter(jnp.dot(inner, down_weight, preferred_element_type=jnp.float32), "head")
        stream = middle + down
    return (stream, jnp.stack(stored))


def solution(mesh):
    return jax.shard_map(
        body,
        mesh=mesh,
        in_specs=(
            P(("seg", "head"), None),
            P("seg"),
            P("seg", None, None),
            P(None, None, "head"),
            P(None, None, "head"),
            P(None, "seg", "head"),
            P(),
            P(),
            P(None, None, "head"),
            P(None, None, "head"),
            P(None, "head", None),
            P(None, None, None, "head"),
            P(None, "head", None),
        ),
        out_specs=(P(("seg", "head"), None), P(None, "seg", None, "head")),
        check_vma=False,
    )
```

```python
import jax
import jax.numpy as jnp
from jax import lax
from jax.sharding import Mesh, PartitionSpec as P

HEADS = 32
KV_HEADS = 8
HD = 64
MEM = 128
SEG_LEN = 512
BLOCK = 128
DEPTH_NUMBER = 2


ROW_AXES = ("sx", "sc")
COLUMN_AXIS = "sy"
SEG_AXES = ("sy", "sx", "sc")


def prefix_weights(rate_all, upto):
    count = rate_all.shape[0]
    order = jnp.arange(count)
    inside = (order[None, :] > order[:, None]) & (order[None, :] < upto)
    span = jnp.prod(jnp.where(inside[:, :, None], rate_all[None, :, :], 1.0), axis=1)
    weight = jnp.where((order < upto)[:, None], span * (1.0 - rate_all), 0.0)
    carry = jnp.prod(jnp.where((order < upto)[:, None], rate_all, 1.0), axis=0)
    return jnp.repeat(weight, HD, axis=1), jnp.repeat(carry, HD)


def ring_pairs(count, step):
    return [(i, (i + step) % count) for i in range(count)]


def ring_gather(piece, axis):
    count = lax.axis_size(axis)
    here = lax.axis_index(axis)
    rows = piece.shape[0]
    half = rows // 2
    ahead = ring_pairs(count, 1)
    behind = ring_pairs(count, -1)
    from_before = lax.ppermute(piece, axis, ahead)
    from_after = lax.ppermute(piece, axis, behind)
    far_top = lax.ppermute(from_before[:half], axis, ahead)
    far_bottom = lax.ppermute(from_after[half:], axis, behind)
    relative = jnp.concatenate([piece, from_after, far_top, far_bottom, from_before], axis=0)
    return jnp.roll(relative, here * rows, axis=0)


def ring_scatter(whole, axis):
    count = lax.axis_size(axis)
    here = lax.axis_index(axis)
    rows = whole.shape[0] // count
    half = rows // 2
    ahead = ring_pairs(count, 1)
    behind = ring_pairs(count, -1)

    def block(offset):
        return lax.dynamic_slice_in_dim(whole, ((here + offset) % count) * rows, rows)

    far = block(2)
    sent_top = lax.ppermute(far[:half].astype(jnp.bfloat16), axis, ahead)
    sent_bottom = lax.ppermute(far[half:].astype(jnp.bfloat16), axis, behind)
    next_part = block(1)
    next_part = jnp.concatenate([next_part[:half] + sent_top.astype(jnp.float32), next_part[half:]])
    prev_part = block(-1)
    prev_part = jnp.concatenate([prev_part[:half], prev_part[half:] + sent_bottom.astype(jnp.float32)])
    got_before = lax.ppermute(next_part.astype(jnp.bfloat16), axis, ahead)
    got_after = lax.ppermute(prev_part.astype(jnp.bfloat16), axis, behind)
    return block(0) + got_before.astype(jnp.float32) + got_after.astype(jnp.float32)


def rms_norm(value, gain):
    factor = lax.rsqrt(jnp.mean(value * value, axis=-1, keepdims=True) + 1e-05)
    return (value * factor * gain).astype(jnp.bfloat16)


def rope_tables(position):
    half = HD // 2
    freq = 500000.0 ** (-(jnp.arange(half).astype(jnp.float32) * 2.0 / HD))
    angle = position.astype(jnp.float32)[:, None] * freq[None, :]
    return (jnp.cos(angle), jnp.sin(angle))


def rotate(tensor, cosine, sine):
    half = tensor.shape[-1] // 2
    first = tensor[..., :half]
    second = tensor[..., half:]
    cos_part = cosine[:, None, :]
    sin_part = sine[:, None, :]
    return jnp.concatenate(
        [first * cos_part - second * sin_part, second * cos_part + first * sin_part], axis=-1
    )


def body(
    tokens,
    document_index,
    block_mask,
    slot_keys,
    mem_init,
    retain,
    attn_gain,
    mlp_gain,
    w_query,
    w_kv,
    w_out,
    w_gate_up,
    w_down,
):
    seg_local = document_index.shape[0] // SEG_LEN
    rows_all = seg_local * SEG_LEN
    cols_query = w_query.shape[2]
    local_heads = cols_query // HD
    group = HEADS // KV_HEADS
    local_kv = local_heads // group
    scale = HD ** (-0.5)
    cosine, sine = rope_tables(jnp.arange(rows_all) % SEG_LEN)
    docs = document_index.reshape(seg_local, SEG_LEN)
    causal = jnp.arange(SEG_LEN)[:, None] >= jnp.arange(SEG_LEN)[None, :]
    stream = tokens
    stored = []
    for layer in range(DEPTH_NUMBER):
        query_weight = w_query[layer]
        pair_weight = w_kv[layer]
        out_weight = w_out[layer]
        widening_matrix = w_gate_up[layer]
        down_weight = w_down[layer]
        normed = rms_norm(stream, attn_gain[layer])
        project_piece = ring_gather(normed, "head")
        projected = jnp.concatenate(
            [
                jnp.dot(project_piece, query_weight, preferred_element_type=jnp.float32),
                jnp.dot(project_piece, pair_weight, preferred_element_type=jnp.float32),
            ],
            axis=1,
        )
        query = rotate(
            projected[:, :cols_query].reshape(rows_all, local_heads, HD), cosine, sine
        ).astype(jnp.bfloat16)
        pairs = projected[:, cols_query:].reshape(rows_all, local_kv, 2, HD)
        lookup_vectors = rotate(pairs[:, :, 0], cosine, sine).astype(jnp.bfloat16)
        values = pairs[:, :, 1].astype(jnp.bfloat16)
        query = query.reshape(seg_local, SEG_LEN, local_kv, group, HD)
        lookup_vectors = lookup_vectors.reshape(seg_local, SEG_LEN, local_kv, HD)
        values = values.reshape(seg_local, SEG_LEN, local_kv, HD)
        slots = slot_keys[layer].reshape(MEM, local_kv, group, HD)
        write_scores = (
            jnp.einsum(
                "mkgd,sjkd->skgmj", slots, lookup_vectors, preferred_element_type=jnp.float32
            )
            * scale
        )
        write_probs = jax.nn.softmax(write_scores, axis=-1).astype(jnp.bfloat16)
        written = jnp.einsum(
            "skgmj,sjkd->smkgd", write_probs, values, preferred_element_type=jnp.float32
        ).reshape(seg_local, MEM, cols_query)
        rates = jnp.repeat(retain[layer], HD, axis=1)[:, None, :]
        here = lax.axis_index(ROW_AXES)
        row = lax.axis_index(COLUMN_AXIS)
        rate_row = rates[0]
        rate_high = rate_row.astype(jnp.bfloat16)
        rest = rate_row - rate_high.astype(jnp.float32)
        rate_mid = rest.astype(jnp.bfloat16)
        rate_low = (rest - rate_mid.astype(jnp.float32)).astype(jnp.bfloat16)
        payload = jnp.concatenate(
            [written[0].astype(jnp.bfloat16), rate_high, rate_mid, rate_low], axis=0
        )
        gathered = lax.all_gather(payload, ROW_AXES)
        written_all = gathered[:, :MEM].astype(jnp.float32)
        rate_parts = gathered[:, MEM:, ::HD].astype(jnp.float32)
        rate_all = rate_parts[:, 0] + rate_parts[:, 1] + rate_parts[:, 2]
        weight, carry = prefix_weights(rate_all, here)
        local = jnp.sum(weight[:, None, :] * written_all, axis=0)
        weight_total, carry_total = prefix_weights(rate_all, rate_all.shape[0])
        total = jnp.sum(weight_total[:, None, :] * written_all, axis=0)
        summary = jnp.concatenate([total, carry_total[None, :]], axis=0)
        row_sums = lax.all_gather(summary, COLUMN_AXIS)
        totals = row_sums[:, :MEM]
        keeps = row_sums[:, MEM, ::HD]
        order = jnp.arange(keeps.shape[0])
        inside = (order[None, :] > order[:, None]) & (order[None, :] < row)
        span = jnp.prod(jnp.where(inside[:, :, None], keeps[None, :, :], 1.0), axis=1)
        row_weight = jnp.repeat(jnp.where((order < row)[:, None], span, 0.0), HD, axis=1)
        row_carry = jnp.repeat(jnp.prod(jnp.where((order < row)[:, None], keeps, 1.0), axis=0), HD)
        entering = row_carry[None, :] * mem_init[layer] + jnp.sum(
            row_weight[:, None, :] * totals, axis=0
        )
        state = carry[None, :] * entering + local
        segment = 0
        memory_read = state.astype(jnp.bfloat16).reshape(MEM, local_kv, group, HD)
        state = rates[segment] * state + (1.0 - rates[segment]) * written[segment]
        after_list = [state]
        blocks = jnp.repeat(jnp.repeat(block_mask[segment], BLOCK, axis=0), BLOCK, axis=1)
        allowed = causal & (docs[segment][:, None] == docs[segment][None, :]) & (blocks == 1)
        slot_scores = (
            jnp.einsum("ikgd,mkgd->kgim", query[segment], slots, preferred_element_type=jnp.float32)
            * scale
        )
        token_scores = (
            jnp.einsum(
                "ikgd,jkd->kgij",
                query[segment],
                lookup_vectors[segment],
                preferred_element_type=jnp.float32,
            )
            * scale
        )
        token_scores = jnp.where(allowed, token_scores, -jnp.inf)
        probs = jax.nn.softmax(
            jnp.concatenate([slot_scores, token_scores], axis=-1), axis=-1
        ).astype(jnp.bfloat16)
        result = jnp.einsum(
            "kgim,mkgd->ikgd", probs[..., :MEM], memory_read, preferred_element_type=jnp.float32
        )
        result = result + jnp.einsum(
            "kgij,jkd->ikgd", probs[..., MEM:], values[segment], preferred_element_type=jnp.float32
        )
        outputs = result.reshape(SEG_LEN, cols_query).astype(jnp.bfloat16)
        stored.append(jnp.stack(after_list))
        mixed = ring_scatter(
            jnp.dot(outputs, out_weight, preferred_element_type=jnp.float32), "head"
        )
        middle = stream + mixed
        both = jnp.einsum(
            "rd,dtf->rtf",
            ring_gather(rms_norm(middle, mlp_gain[layer]), "head"),
            widening_matrix,
            preferred_element_type=jnp.float32,
        )
        inner = (jax.nn.silu(both[:, 0]) * both[:, 1]).astype(jnp.bfloat16)
        down = ring_scatter(jnp.dot(inner, down_weight, preferred_element_type=jnp.float32), "head")
        stream = middle + down
    return (stream, jnp.stack(stored))


def solution(mesh):
    seg_size = mesh.shape["seg"]
    head_size = mesh.shape["head"]
    fine = Mesh(
        mesh.devices.reshape(seg_size // 8, 4, 2, head_size), SEG_AXES + ("head",)
    )
    return jax.shard_map(
        body,
        mesh=fine,
        in_specs=(
            P(SEG_AXES + ("head",), None),
            P(SEG_AXES),
            P(SEG_AXES, None, None),
            P(None, None, "head"),
            P(None, None, "head"),
            P(None, SEG_AXES, "head"),
            P(),
            P(),
            P(None, None, "head"),
            P(None, None, "head"),
            P(None, "head", None),
            P(None, None, None, "head"),
            P(None, "head", None),
        ),
        out_specs=(P(SEG_AXES + ("head",), None), P(None, SEG_AXES, None, "head")),
        check_vma=False,
    )
```

```python
import jax
import jax.numpy as jnp
from jax import lax
from jax.sharding import PartitionSpec as P

HEADS = 32
KV_HEADS = 8
HD = 64
MEM = 128
SEG_LEN = 512
BLOCK = 128
DEPTH_NUMBER = 2


def ring_pairs(count, step):
    return [(i, (i + step) % count) for i in range(count)]


def ring_gather(piece, axis):
    count = lax.axis_size(axis)
    here = lax.axis_index(axis)
    rows = piece.shape[0]
    half = rows // 2
    ahead = ring_pairs(count, 1)
    behind = ring_pairs(count, -1)
    from_before = lax.ppermute(piece, axis, ahead)
    from_after = lax.ppermute(piece, axis, behind)
    far_top = lax.ppermute(from_before[:half], axis, ahead)
    far_bottom = lax.ppermute(from_after[half:], axis, behind)
    relative = jnp.concatenate([piece, from_after, far_top, far_bottom, from_before], axis=0)
    return jnp.roll(relative, here * rows, axis=0)


def ring_scatter(whole, axis):
    count = lax.axis_size(axis)
    here = lax.axis_index(axis)
    rows = whole.shape[0] // count
    half = rows // 2
    ahead = ring_pairs(count, 1)
    behind = ring_pairs(count, -1)

    def block(offset):
        return lax.dynamic_slice_in_dim(whole, ((here + offset) % count) * rows, rows)

    far = block(2)
    sent_top = lax.ppermute(far[:half].astype(jnp.bfloat16), axis, ahead)
    sent_bottom = lax.ppermute(far[half:].astype(jnp.bfloat16), axis, behind)
    next_part = block(1)
    next_part = jnp.concatenate([next_part[:half] + sent_top.astype(jnp.float32), next_part[half:]])
    prev_part = block(-1)
    prev_part = jnp.concatenate([prev_part[:half], prev_part[half:] + sent_bottom.astype(jnp.float32)])
    got_before = lax.ppermute(next_part.astype(jnp.bfloat16), axis, ahead)
    got_after = lax.ppermute(prev_part.astype(jnp.bfloat16), axis, behind)
    return block(0) + got_before.astype(jnp.float32) + got_after.astype(jnp.float32)


def ring_pieces(piece, axis):
    count = lax.axis_size(axis)
    rows = piece.shape[0]
    half = rows // 2
    ahead = ring_pairs(count, 1)
    behind = ring_pairs(count, -1)
    from_before = lax.ppermute(piece, axis, ahead)
    from_after = lax.ppermute(piece, axis, behind)
    far_top = lax.ppermute(from_before[:half], axis, ahead)
    far_bottom = lax.ppermute(from_after[half:], axis, behind)
    return from_before, from_after, jnp.concatenate([far_top, far_bottom], axis=0)


def ring_scatter_parts(own, next_part, prev_part, far, axis):
    count = lax.axis_size(axis)
    half = own.shape[0] // 2
    ahead = ring_pairs(count, 1)
    behind = ring_pairs(count, -1)
    sent_top = lax.ppermute(far[:half].astype(jnp.bfloat16), axis, ahead)
    sent_bottom = lax.ppermute(far[half:].astype(jnp.bfloat16), axis, behind)
    next_part = jnp.concatenate([next_part[:half] + sent_top.astype(jnp.float32), next_part[half:]])
    prev_part = jnp.concatenate([prev_part[:half], prev_part[half:] + sent_bottom.astype(jnp.float32)])
    got_before = lax.ppermute(next_part.astype(jnp.bfloat16), axis, ahead)
    got_after = lax.ppermute(prev_part.astype(jnp.bfloat16), axis, behind)
    return own + got_before.astype(jnp.float32) + got_after.astype(jnp.float32)


def feed_forward(rows, widening_matrix, down_weight):
    both = jnp.einsum("rd,dtf->rtf", rows, widening_matrix, preferred_element_type=jnp.float32)
    inner = (jax.nn.silu(both[:, 0]) * both[:, 1]).astype(jnp.bfloat16)
    return jnp.dot(inner, down_weight, preferred_element_type=jnp.float32)


def rms_norm(value, gain):
    factor = lax.rsqrt(jnp.mean(value * value, axis=-1, keepdims=True) + 1e-05)
    return (value * factor * gain).astype(jnp.bfloat16)


def rope_tables(position):
    half = HD // 2
    freq = 500000.0 ** (-(jnp.arange(half).astype(jnp.float32) * 2.0 / HD))
    angle = position.astype(jnp.float32)[:, None] * freq[None, :]
    return (jnp.cos(angle), jnp.sin(angle))


def rotate(tensor, cosine, sine):
    half = tensor.shape[-1] // 2
    first = tensor[..., :half]
    second = tensor[..., half:]
    cos_part = cosine[:, None, :]
    sin_part = sine[:, None, :]
    return jnp.concatenate(
        [first * cos_part - second * sin_part, second * cos_part + first * sin_part], axis=-1
    )


def body(
    tokens,
    document_index,
    block_mask,
    slot_keys,
    mem_init,
    retain,
    attn_gain,
    mlp_gain,
    w_query,
    w_kv,
    w_out,
    w_gate_up,
    w_down,
):
    seg_local = document_index.shape[0] // SEG_LEN
    rows_all = seg_local * SEG_LEN
    cols_query = w_query.shape[2]
    local_heads = cols_query // HD
    group = HEADS // KV_HEADS
    local_kv = local_heads // group
    scale = HD ** (-0.5)
    cosine, sine = rope_tables(jnp.arange(rows_all) % SEG_LEN)
    docs = document_index.reshape(seg_local, SEG_LEN)
    causal = jnp.arange(SEG_LEN)[:, None] >= jnp.arange(SEG_LEN)[None, :]
    stream = tokens
    stored = []
    for layer in range(DEPTH_NUMBER):
        query_weight = w_query[layer]
        pair_weight = w_kv[layer]
        out_weight = w_out[layer]
        down_weight = w_down[layer]
        normed = rms_norm(stream, attn_gain[layer])
        project_piece = ring_gather(normed, "head")
        projected = jnp.concatenate(
            [
                jnp.dot(project_piece, query_weight, preferred_element_type=jnp.float32),
                jnp.dot(project_piece, pair_weight, preferred_element_type=jnp.float32),
            ],
            axis=1,
        )
        query = rotate(
            projected[:, :cols_query].reshape(rows_all, local_heads, HD), cosine, sine
        ).astype(jnp.bfloat16)
        pairs = projected[:, cols_query:].reshape(rows_all, local_kv, 2, HD)
        lookup_vectors = rotate(pairs[:, :, 0], cosine, sine).astype(jnp.bfloat16)
        values = pairs[:, :, 1].astype(jnp.bfloat16)
        query = query.reshape(seg_local, SEG_LEN, local_kv, group, HD)
        lookup_vectors = lookup_vectors.reshape(seg_local, SEG_LEN, local_kv, HD)
        values = values.reshape(seg_local, SEG_LEN, local_kv, HD)
        slots = slot_keys[layer].reshape(MEM, local_kv, group, HD)
        write_scores = (
            jnp.einsum(
                "mkgd,sjkd->skgmj", slots, lookup_vectors, preferred_element_type=jnp.float32
            )
            * scale
        )
        write_probs = jax.nn.softmax(write_scores, axis=-1).astype(jnp.bfloat16)
        written = jnp.einsum(
            "skgmj,sjkd->smkgd", write_probs, values, preferred_element_type=jnp.float32
        ).reshape(seg_local, MEM, cols_query)
        rates = jnp.repeat(retain[layer], HD, axis=1)[:, None, :]
        here = lax.axis_index("seg")
        count = lax.axis_size("seg")
        rate_row = rates[0]
        rate_high = rate_row.astype(jnp.bfloat16)
        rest = rate_row - rate_high.astype(jnp.float32)
        rate_mid = rest.astype(jnp.bfloat16)
        rate_low = (rest - rate_mid.astype(jnp.float32)).astype(jnp.bfloat16)
        payload = jnp.concatenate(
            [written[0].astype(jnp.bfloat16), rate_high, rate_mid, rate_low], axis=0
        )
        gathered = lax.all_gather(payload, "seg")
        if layer == 0:
            gathered, gate_up_slices = lax.optimization_barrier(
                (gathered, [w_gate_up[index] for index in range(DEPTH_NUMBER)])
            )
        written_all = gathered[:, :MEM].astype(jnp.float32)
        rate_parts = gathered[:, MEM:, ::HD].astype(jnp.float32)
        rate_all = rate_parts[:, 0] + rate_parts[:, 1] + rate_parts[:, 2]
        order = jnp.arange(count)
        inside = (order[None, :] > order[:, None]) & (order[None, :] < here)
        span = jnp.prod(jnp.where(inside[:, :, None], rate_all[None, :, :], 1.0), axis=1)
        weight = jnp.where((order < here)[:, None], span * (1.0 - rate_all), 0.0)
        carry = jnp.prod(jnp.where((order < here)[:, None], rate_all, 1.0), axis=0)
        weight = jnp.repeat(weight, HD, axis=1)
        carry = jnp.repeat(carry, HD)
        state = carry[None, :] * mem_init[layer] + jnp.sum(
            weight[:, None, :] * written_all, axis=0
        )
        segment = 0
        memory_read = state.astype(jnp.bfloat16).reshape(MEM, local_kv, group, HD)
        state = rates[segment] * state + (1.0 - rates[segment]) * written[segment]
        after_list = [state]
        blocks = jnp.repeat(jnp.repeat(block_mask[segment], BLOCK, axis=0), BLOCK, axis=1)
        allowed = causal & (docs[segment][:, None] == docs[segment][None, :]) & (blocks == 1)
        slot_scores = (
            jnp.einsum("ikgd,mkgd->kgim", query[segment], slots, preferred_element_type=jnp.float32)
            * scale
        )
        token_scores = (
            jnp.einsum(
                "ikgd,jkd->kgij",
                query[segment],
                lookup_vectors[segment],
                preferred_element_type=jnp.float32,
            )
            * scale
        )
        token_scores = jnp.where(allowed, token_scores, -jnp.inf)
        probs = jax.nn.softmax(
            jnp.concatenate([slot_scores, token_scores], axis=-1), axis=-1
        ).astype(jnp.bfloat16)
        result = jnp.einsum(
            "kgim,mkgd->ikgd", probs[..., :MEM], memory_read, preferred_element_type=jnp.float32
        )
        result = result + jnp.einsum(
            "kgij,jkd->ikgd", probs[..., MEM:], values[segment], preferred_element_type=jnp.float32
        )
        outputs = result.reshape(SEG_LEN, cols_query).astype(jnp.bfloat16)
        stored.append(jnp.stack(after_list))
        mixed = ring_scatter(
            jnp.dot(outputs, out_weight, preferred_element_type=jnp.float32), "head"
        )
        middle = stream + mixed
        mlp_piece = rms_norm(middle, mlp_gain[layer])
        from_before, from_after, far_rows = ring_pieces(mlp_piece, "head")
        widening_matrix = gate_up_slices[layer]
        own_part = feed_forward(mlp_piece, widening_matrix, down_weight)
        side_parts = feed_forward(
            jnp.concatenate([from_before, from_after], axis=0), widening_matrix, down_weight
        )
        far_part = feed_forward(far_rows, widening_matrix, down_weight)
        piece_rows = mlp_piece.shape[0]
        down = ring_scatter_parts(
            own_part, side_parts[piece_rows:], side_parts[:piece_rows], far_part, "head"
        )
        stream = middle + down
    return (stream, jnp.stack(stored))


def solution(mesh):
    return jax.shard_map(
        body,
        mesh=mesh,
        in_specs=(
            P(("seg", "head"), None),
            P("seg"),
            P("seg", None, None),
            P(None, None, "head"),
            P(None, None, "head"),
            P(None, "seg", "head"),
            P(),
            P(),
            P(None, None, "head"),
            P(None, None, "head"),
            P(None, "head", None),
            P(None, None, None, "head"),
            P(None, "head", None),
        ),
        out_specs=(P(("seg", "head"), None), P(None, "seg", None, "head")),
        check_vma=False,
    )
```

```python
import jax
import jax.numpy as jnp
from jax import lax
from jax.sharding import PartitionSpec as P

HEADS = 32
KV_HEADS = 8
HD = 64
MEM = 128
SEG_LEN = 512
BLOCK = 128
DEPTH_NUMBER = 2


def ring_pairs(count, step):
    return [(i, (i + step) % count) for i in range(count)]


def ring_gather(piece, axis):
    count = lax.axis_size(axis)
    here = lax.axis_index(axis)
    rows = piece.shape[0]
    half = rows // 2
    ahead = ring_pairs(count, 1)
    behind = ring_pairs(count, -1)
    from_before = lax.ppermute(piece, axis, ahead)
    from_after = lax.ppermute(piece, axis, behind)
    far_top = lax.ppermute(from_before[:half], axis, ahead)
    far_bottom = lax.ppermute(from_after[half:], axis, behind)
    relative = jnp.concatenate([piece, from_after, far_top, far_bottom, from_before], axis=0)
    return jnp.roll(relative, here * rows, axis=0)


def ring_scatter(whole, axis):
    count = lax.axis_size(axis)
    here = lax.axis_index(axis)
    rows = whole.shape[0] // count
    half = rows // 2
    ahead = ring_pairs(count, 1)
    behind = ring_pairs(count, -1)

    def block(offset):
        return lax.dynamic_slice_in_dim(whole, ((here + offset) % count) * rows, rows)

    far = block(2)
    sent_top = lax.ppermute(far[:half].astype(jnp.bfloat16), axis, ahead)
    sent_bottom = lax.ppermute(far[half:].astype(jnp.bfloat16), axis, behind)
    next_part = block(1)
    next_part = jnp.concatenate([next_part[:half] + sent_top.astype(jnp.float32), next_part[half:]])
    prev_part = block(-1)
    prev_part = jnp.concatenate([prev_part[:half], prev_part[half:] + sent_bottom.astype(jnp.float32)])
    got_before = lax.ppermute(next_part.astype(jnp.bfloat16), axis, ahead)
    got_after = lax.ppermute(prev_part.astype(jnp.bfloat16), axis, behind)
    return block(0) + got_before.astype(jnp.float32) + got_after.astype(jnp.float32)


def ring_pieces(piece, axis):
    count = lax.axis_size(axis)
    rows = piece.shape[0]
    half = rows // 2
    ahead = ring_pairs(count, 1)
    behind = ring_pairs(count, -1)
    from_before = lax.ppermute(piece, axis, ahead)
    from_after = lax.ppermute(piece, axis, behind)
    far_top = lax.ppermute(from_before[:half], axis, ahead)
    far_bottom = lax.ppermute(from_after[half:], axis, behind)
    return from_before, from_after, jnp.concatenate([far_top, far_bottom], axis=0)


def ring_scatter_parts(own, next_part, prev_part, far, axis):
    count = lax.axis_size(axis)
    half = own.shape[0] // 2
    ahead = ring_pairs(count, 1)
    behind = ring_pairs(count, -1)
    sent_top = lax.ppermute(far[:half].astype(jnp.bfloat16), axis, ahead)
    sent_bottom = lax.ppermute(far[half:].astype(jnp.bfloat16), axis, behind)
    next_part = jnp.concatenate([next_part[:half] + sent_top.astype(jnp.float32), next_part[half:]])
    prev_part = jnp.concatenate([prev_part[:half], prev_part[half:] + sent_bottom.astype(jnp.float32)])
    got_before = lax.ppermute(next_part.astype(jnp.bfloat16), axis, ahead)
    got_after = lax.ppermute(prev_part.astype(jnp.bfloat16), axis, behind)
    return own + got_before.astype(jnp.float32) + got_after.astype(jnp.float32)


def feed_forward(rows, widening_matrix, down_weight):
    both = jnp.einsum("rd,dtf->rtf", rows, widening_matrix, preferred_element_type=jnp.float32)
    inner = (jax.nn.silu(both[:, 0]) * both[:, 1]).astype(jnp.bfloat16)
    return jnp.dot(inner, down_weight, preferred_element_type=jnp.float32)


def rms_norm(value, gain):
    factor = lax.rsqrt(jnp.mean(value * value, axis=-1, keepdims=True) + 1e-05)
    return (value * factor * gain).astype(jnp.bfloat16)


def rope_tables(position):
    half = HD // 2
    freq = 500000.0 ** (-(jnp.arange(half).astype(jnp.float32) * 2.0 / HD))
    angle = position.astype(jnp.float32)[:, None] * freq[None, :]
    return (jnp.cos(angle), jnp.sin(angle))


def rotate(tensor, cosine, sine):
    half = tensor.shape[-1] // 2
    first = tensor[..., :half]
    second = tensor[..., half:]
    cos_part = cosine[:, None, :]
    sin_part = sine[:, None, :]
    return jnp.concatenate(
        [first * cos_part - second * sin_part, second * cos_part + first * sin_part], axis=-1
    )


def body(
    tokens,
    document_index,
    block_mask,
    slot_keys,
    mem_init,
    retain,
    attn_gain,
    mlp_gain,
    w_query,
    w_kv,
    w_out,
    w_gate_up,
    w_down,
):
    seg_local = document_index.shape[0] // SEG_LEN
    rows_all = seg_local * SEG_LEN
    cols_query = w_query.shape[2]
    local_heads = cols_query // HD
    group = HEADS // KV_HEADS
    local_kv = local_heads // group
    scale = HD ** (-0.5)
    cosine, sine = rope_tables(jnp.arange(rows_all) % SEG_LEN)
    docs = document_index.reshape(seg_local, SEG_LEN)
    causal = jnp.arange(SEG_LEN)[:, None] >= jnp.arange(SEG_LEN)[None, :]
    stream = tokens
    stored = []
    for layer in range(DEPTH_NUMBER):
        query_weight = w_query[layer]
        pair_weight = w_kv[layer]
        out_weight = w_out[layer]
        down_weight = w_down[layer]
        normed = rms_norm(stream, attn_gain[layer])
        project_piece = ring_gather(normed, "head")
        if layer == 0:
            project_piece, gate_up_slices = lax.optimization_barrier(
                (project_piece, [w_gate_up[index] for index in range(DEPTH_NUMBER)])
            )
        projected = jnp.concatenate(
            [
                jnp.dot(project_piece, query_weight, preferred_element_type=jnp.float32),
                jnp.dot(project_piece, pair_weight, preferred_element_type=jnp.float32),
            ],
            axis=1,
        )
        query = rotate(
            projected[:, :cols_query].reshape(rows_all, local_heads, HD), cosine, sine
        ).astype(jnp.bfloat16)
        pairs = projected[:, cols_query:].reshape(rows_all, local_kv, 2, HD)
        lookup_vectors = rotate(pairs[:, :, 0], cosine, sine).astype(jnp.bfloat16)
        values = pairs[:, :, 1].astype(jnp.bfloat16)
        query = query.reshape(seg_local, SEG_LEN, local_kv, group, HD)
        lookup_vectors = lookup_vectors.reshape(seg_local, SEG_LEN, local_kv, HD)
        values = values.reshape(seg_local, SEG_LEN, local_kv, HD)
        slots = slot_keys[layer].reshape(MEM, local_kv, group, HD)
        write_scores = (
            jnp.einsum(
                "mkgd,sjkd->skgmj", slots, lookup_vectors, preferred_element_type=jnp.float32
            )
            * scale
        )
        write_probs = jax.nn.softmax(write_scores, axis=-1).astype(jnp.bfloat16)
        written = jnp.einsum(
            "skgmj,sjkd->smkgd", write_probs, values, preferred_element_type=jnp.float32
        ).reshape(seg_local, MEM, cols_query)
        rates = jnp.repeat(retain[layer], HD, axis=1)[:, None, :]
        here = lax.axis_index("seg")
        count = lax.axis_size("seg")
        rate_row = rates[0]
        rate_high = rate_row.astype(jnp.bfloat16)
        rest = rate_row - rate_high.astype(jnp.float32)
        rate_mid = rest.astype(jnp.bfloat16)
        rate_low = (rest - rate_mid.astype(jnp.float32)).astype(jnp.bfloat16)
        payload = jnp.concatenate(
            [written[0].astype(jnp.bfloat16), rate_high, rate_mid, rate_low], axis=0
        )
        gathered = lax.all_gather(payload, "seg")
        written_all = gathered[:, :MEM].astype(jnp.float32)
        rate_parts = gathered[:, MEM:, ::HD].astype(jnp.float32)
        rate_all = rate_parts[:, 0] + rate_parts[:, 1] + rate_parts[:, 2]
        order = jnp.arange(count)
        inside = (order[None, :] > order[:, None]) & (order[None, :] < here)
        span = jnp.prod(jnp.where(inside[:, :, None], rate_all[None, :, :], 1.0), axis=1)
        weight = jnp.where((order < here)[:, None], span * (1.0 - rate_all), 0.0)
        carry = jnp.prod(jnp.where((order < here)[:, None], rate_all, 1.0), axis=0)
        weight = jnp.repeat(weight, HD, axis=1)
        carry = jnp.repeat(carry, HD)
        state = carry[None, :] * mem_init[layer] + jnp.sum(
            weight[:, None, :] * written_all, axis=0
        )
        segment = 0
        memory_read = state.astype(jnp.bfloat16).reshape(MEM, local_kv, group, HD)
        state = rates[segment] * state + (1.0 - rates[segment]) * written[segment]
        after_list = [state]
        blocks = jnp.repeat(jnp.repeat(block_mask[segment], BLOCK, axis=0), BLOCK, axis=1)
        allowed = causal & (docs[segment][:, None] == docs[segment][None, :]) & (blocks == 1)
        slot_scores = (
            jnp.einsum("ikgd,mkgd->kgim", query[segment], slots, preferred_element_type=jnp.float32)
            * scale
        )
        token_scores = (
            jnp.einsum(
                "ikgd,jkd->kgij",
                query[segment],
                lookup_vectors[segment],
                preferred_element_type=jnp.float32,
            )
            * scale
        )
        token_scores = jnp.where(allowed, token_scores, -jnp.inf)
        probs = jax.nn.softmax(
            jnp.concatenate([slot_scores, token_scores], axis=-1), axis=-1
        ).astype(jnp.bfloat16)
        result = jnp.einsum(
            "kgim,mkgd->ikgd", probs[..., :MEM], memory_read, preferred_element_type=jnp.float32
        )
        result = result + jnp.einsum(
            "kgij,jkd->ikgd", probs[..., MEM:], values[segment], preferred_element_type=jnp.float32
        )
        outputs = result.reshape(SEG_LEN, cols_query).astype(jnp.bfloat16)
        stored.append(jnp.stack(after_list))
        mixed = ring_scatter(
            jnp.dot(outputs, out_weight, preferred_element_type=jnp.float32), "head"
        )
        middle = stream + mixed
        mlp_piece = rms_norm(middle, mlp_gain[layer])
        from_before, from_after, far_rows = ring_pieces(mlp_piece, "head")
        widening_matrix = gate_up_slices[layer]
        own_part = feed_forward(mlp_piece, widening_matrix, down_weight)
        side_parts = feed_forward(
            jnp.concatenate([from_before, from_after], axis=0), widening_matrix, down_weight
        )
        far_part = feed_forward(far_rows, widening_matrix, down_weight)
        piece_rows = mlp_piece.shape[0]
        down = ring_scatter_parts(
            own_part, side_parts[piece_rows:], side_parts[:piece_rows], far_part, "head"
        )
        stream = middle + down
    return (stream, jnp.stack(stored))


def solution(mesh):
    return jax.shard_map(
        body,
        mesh=mesh,
        in_specs=(
            P(("seg", "head"), None),
            P("seg"),
            P("seg", None, None),
            P(None, None, "head"),
            P(None, None, "head"),
            P(None, "seg", "head"),
            P(),
            P(),
            P(None, None, "head"),
            P(None, None, "head"),
            P(None, "head", None),
            P(None, None, None, "head"),
            P(None, "head", None),
        ),
        out_specs=(P(("seg", "head"), None), P(None, "seg", None, "head")),
        check_vma=False,
    )
```

```python
import jax
import jax.numpy as jnp
from jax import lax
from jax.sharding import PartitionSpec as P

HEADS = 32
KV_HEADS = 8
HD = 64
MEM = 128
SEG_LEN = 512
BLOCK = 128
DEPTH_NUMBER = 2


def ring_pairs(count, step):
    return [(i, (i + step) % count) for i in range(count)]


def ring_gather(piece, axis):
    count = lax.axis_size(axis)
    here = lax.axis_index(axis)
    rows = piece.shape[0]
    half = rows // 2
    ahead = ring_pairs(count, 1)
    behind = ring_pairs(count, -1)
    from_before = lax.ppermute(piece, axis, ahead)
    from_after = lax.ppermute(piece, axis, behind)
    far_top = lax.ppermute(from_before[:half], axis, ahead)
    far_bottom = lax.ppermute(from_after[half:], axis, behind)
    relative = jnp.concatenate([piece, from_after, far_top, far_bottom, from_before], axis=0)
    return jnp.roll(relative, here * rows, axis=0)


def ring_scatter(whole, axis):
    count = lax.axis_size(axis)
    here = lax.axis_index(axis)
    rows = whole.shape[0] // count
    half = rows // 2
    ahead = ring_pairs(count, 1)
    behind = ring_pairs(count, -1)

    def block(offset):
        return lax.dynamic_slice_in_dim(whole, ((here + offset) % count) * rows, rows)

    far = block(2)
    sent_top = lax.ppermute(far[:half].astype(jnp.bfloat16), axis, ahead)
    sent_bottom = lax.ppermute(far[half:].astype(jnp.bfloat16), axis, behind)
    next_part = block(1)
    next_part = jnp.concatenate([next_part[:half] + sent_top.astype(jnp.float32), next_part[half:]])
    prev_part = block(-1)
    prev_part = jnp.concatenate([prev_part[:half], prev_part[half:] + sent_bottom.astype(jnp.float32)])
    got_before = lax.ppermute(next_part.astype(jnp.bfloat16), axis, ahead)
    got_after = lax.ppermute(prev_part.astype(jnp.bfloat16), axis, behind)
    return block(0) + got_before.astype(jnp.float32) + got_after.astype(jnp.float32)


def ring_pieces(piece, axis):
    count = lax.axis_size(axis)
    rows = piece.shape[0]
    half = rows // 2
    ahead = ring_pairs(count, 1)
    behind = ring_pairs(count, -1)
    from_before = lax.ppermute(piece, axis, ahead)
    from_after = lax.ppermute(piece, axis, behind)
    far_top = lax.ppermute(from_before[:half], axis, ahead)
    far_bottom = lax.ppermute(from_after[half:], axis, behind)
    return from_before, from_after, jnp.concatenate([far_top, far_bottom], axis=0)


def ring_scatter_parts(own, next_part, prev_part, far, axis):
    count = lax.axis_size(axis)
    half = own.shape[0] // 2
    ahead = ring_pairs(count, 1)
    behind = ring_pairs(count, -1)
    sent_top = lax.ppermute(far[:half].astype(jnp.bfloat16), axis, ahead)
    sent_bottom = lax.ppermute(far[half:].astype(jnp.bfloat16), axis, behind)
    next_part = jnp.concatenate([next_part[:half] + sent_top.astype(jnp.float32), next_part[half:]])
    prev_part = jnp.concatenate([prev_part[:half], prev_part[half:] + sent_bottom.astype(jnp.float32)])
    got_before = lax.ppermute(next_part.astype(jnp.bfloat16), axis, ahead)
    got_after = lax.ppermute(prev_part.astype(jnp.bfloat16), axis, behind)
    return own + got_before.astype(jnp.float32) + got_after.astype(jnp.float32)


def feed_forward(rows, widening_matrix, down_weight):
    both = jnp.einsum("rd,dtf->rtf", rows, widening_matrix, preferred_element_type=jnp.float32)
    inner = (jax.nn.silu(both[:, 0]) * both[:, 1]).astype(jnp.bfloat16)
    return jnp.dot(inner, down_weight, preferred_element_type=jnp.float32)


def rms_norm(value, gain):
    factor = lax.rsqrt(jnp.mean(value * value, axis=-1, keepdims=True) + 1e-05)
    return (value * factor * gain).astype(jnp.bfloat16)


def rope_tables(position):
    half = HD // 2
    freq = 500000.0 ** (-(jnp.arange(half).astype(jnp.float32) * 2.0 / HD))
    angle = position.astype(jnp.float32)[:, None] * freq[None, :]
    return (jnp.cos(angle), jnp.sin(angle))


def rotate(tensor, cosine, sine):
    half = tensor.shape[-1] // 2
    first = tensor[..., :half]
    second = tensor[..., half:]
    cos_part = cosine[:, None, :]
    sin_part = sine[:, None, :]
    return jnp.concatenate(
        [first * cos_part - second * sin_part, second * cos_part + first * sin_part], axis=-1
    )


def body(
    tokens,
    document_index,
    block_mask,
    slot_keys,
    mem_init,
    retain,
    attn_gain,
    mlp_gain,
    w_query,
    w_kv,
    w_out,
    w_gate_up,
    w_down,
):
    seg_local = document_index.shape[0] // SEG_LEN
    rows_all = seg_local * SEG_LEN
    cols_query = w_query.shape[2]
    local_heads = cols_query // HD
    group = HEADS // KV_HEADS
    local_kv = local_heads // group
    scale = HD ** (-0.5)
    cosine, sine = rope_tables(jnp.arange(rows_all) % SEG_LEN)
    docs = document_index.reshape(seg_local, SEG_LEN)
    causal = jnp.arange(SEG_LEN)[:, None] >= jnp.arange(SEG_LEN)[None, :]
    stream = tokens
    stored = []
    for layer in range(DEPTH_NUMBER):
        query_weight = w_query[layer]
        pair_weight = w_kv[layer]
        out_weight = w_out[layer]
        down_weight = w_down[layer]
        normed = rms_norm(stream, attn_gain[layer])
        project_piece = ring_gather(normed, "head")
        if layer == 0:
            project_piece, gate_up_slices = lax.optimization_barrier(
                (project_piece, [w_gate_up[index] for index in range(DEPTH_NUMBER)])
            )
        pairs = jnp.dot(
            project_piece, pair_weight, preferred_element_type=jnp.float32
        ).reshape(rows_all, local_kv, 2, HD)
        lookup_vectors = rotate(pairs[:, :, 0], cosine, sine).astype(jnp.bfloat16)
        values = pairs[:, :, 1].astype(jnp.bfloat16)
        query = rotate(
            jnp.dot(project_piece, query_weight, preferred_element_type=jnp.float32).reshape(
                rows_all, local_heads, HD
            ),
            cosine,
            sine,
        ).astype(jnp.bfloat16)
        query = query.reshape(seg_local, SEG_LEN, local_kv, group, HD)
        lookup_vectors = lookup_vectors.reshape(seg_local, SEG_LEN, local_kv, HD)
        values = values.reshape(seg_local, SEG_LEN, local_kv, HD)
        slots = slot_keys[layer].reshape(MEM, local_kv, group, HD)
        write_scores = (
            jnp.einsum(
                "mkgd,sjkd->skgmj", slots, lookup_vectors, preferred_element_type=jnp.float32
            )
            * scale
        )
        write_probs = jax.nn.softmax(write_scores, axis=-1).astype(jnp.bfloat16)
        written = jnp.einsum(
            "skgmj,sjkd->smkgd", write_probs, values, preferred_element_type=jnp.float32
        ).reshape(seg_local, MEM, cols_query)
        rates = jnp.repeat(retain[layer], HD, axis=1)[:, None, :]
        here = lax.axis_index("seg")
        count = lax.axis_size("seg")
        rate_row = rates[0]
        rate_high = rate_row.astype(jnp.bfloat16)
        rest = rate_row - rate_high.astype(jnp.float32)
        rate_mid = rest.astype(jnp.bfloat16)
        rate_low = (rest - rate_mid.astype(jnp.float32)).astype(jnp.bfloat16)
        payload = jnp.concatenate(
            [written[0].astype(jnp.bfloat16), rate_high, rate_mid, rate_low], axis=0
        )
        gathered = lax.all_gather(payload, "seg")
        written_all = gathered[:, :MEM].astype(jnp.float32)
        rate_parts = gathered[:, MEM:, ::HD].astype(jnp.float32)
        rate_all = rate_parts[:, 0] + rate_parts[:, 1] + rate_parts[:, 2]
        order = jnp.arange(count)
        inside = (order[None, :] > order[:, None]) & (order[None, :] < here)
        span = jnp.prod(jnp.where(inside[:, :, None], rate_all[None, :, :], 1.0), axis=1)
        weight = jnp.where((order < here)[:, None], span * (1.0 - rate_all), 0.0)
        carry = jnp.prod(jnp.where((order < here)[:, None], rate_all, 1.0), axis=0)
        weight = jnp.repeat(weight, HD, axis=1)
        carry = jnp.repeat(carry, HD)
        state = carry[None, :] * mem_init[layer] + jnp.sum(
            weight[:, None, :] * written_all, axis=0
        )
        segment = 0
        memory_read = state.astype(jnp.bfloat16).reshape(MEM, local_kv, group, HD)
        state = rates[segment] * state + (1.0 - rates[segment]) * written[segment]
        after_list = [state]
        blocks = jnp.repeat(jnp.repeat(block_mask[segment], BLOCK, axis=0), BLOCK, axis=1)
        allowed = causal & (docs[segment][:, None] == docs[segment][None, :]) & (blocks == 1)
        slot_scores = (
            jnp.einsum("ikgd,mkgd->kgim", query[segment], slots, preferred_element_type=jnp.float32)
            * scale
        )
        token_scores = (
            jnp.einsum(
                "ikgd,jkd->kgij",
                query[segment],
                lookup_vectors[segment],
                preferred_element_type=jnp.float32,
            )
            * scale
        )
        token_scores = jnp.where(allowed, token_scores, -jnp.inf)
        probs = jax.nn.softmax(
            jnp.concatenate([slot_scores, token_scores], axis=-1), axis=-1
        ).astype(jnp.bfloat16)
        result = jnp.einsum(
            "kgim,mkgd->ikgd", probs[..., :MEM], memory_read, preferred_element_type=jnp.float32
        )
        result = result + jnp.einsum(
            "kgij,jkd->ikgd", probs[..., MEM:], values[segment], preferred_element_type=jnp.float32
        )
        outputs = result.reshape(SEG_LEN, cols_query).astype(jnp.bfloat16)
        stored.append(jnp.stack(after_list))
        mixed = ring_scatter(
            jnp.dot(outputs, out_weight, preferred_element_type=jnp.float32), "head"
        )
        middle = stream + mixed
        mlp_piece = rms_norm(middle, mlp_gain[layer])
        from_before, from_after, far_rows = ring_pieces(mlp_piece, "head")
        widening_matrix = gate_up_slices[layer]
        own_part = feed_forward(mlp_piece, widening_matrix, down_weight)
        side_parts = feed_forward(
            jnp.concatenate([from_before, from_after], axis=0), widening_matrix, down_weight
        )
        far_part = feed_forward(far_rows, widening_matrix, down_weight)
        piece_rows = mlp_piece.shape[0]
        down = ring_scatter_parts(
            own_part, side_parts[piece_rows:], side_parts[:piece_rows], far_part, "head"
        )
        stream = middle + down
    return (stream, jnp.stack(stored))


def solution(mesh):
    return jax.shard_map(
        body,
        mesh=mesh,
        in_specs=(
            P(("seg", "head"), None),
            P("seg"),
            P("seg", None, None),
            P(None, None, "head"),
            P(None, None, "head"),
            P(None, "seg", "head"),
            P(),
            P(),
            P(None, None, "head"),
            P(None, None, "head"),
            P(None, "head", None),
            P(None, None, None, "head"),
            P(None, "head", None),
        ),
        out_specs=(P(("seg", "head"), None), P(None, "seg", None, "head")),
        check_vma=False,
    )
```

```python
import jax
import jax.numpy as jnp
from jax import lax
from jax.sharding import PartitionSpec as P

HEADS = 32
KV_HEADS = 8
HD = 64
MEM = 128
SEG_LEN = 512
BLOCK = 128
DEPTH_NUMBER = 2


def ring_pairs(count, step):
    return [(i, (i + step) % count) for i in range(count)]


def ring_gather(piece, axis):
    count = lax.axis_size(axis)
    here = lax.axis_index(axis)
    rows = piece.shape[0]
    half = rows // 2
    ahead = ring_pairs(count, 1)
    behind = ring_pairs(count, -1)
    from_before = lax.ppermute(piece, axis, ahead)
    from_after = lax.ppermute(piece, axis, behind)
    far_top = lax.ppermute(from_before[:half], axis, ahead)
    far_bottom = lax.ppermute(from_after[half:], axis, behind)
    relative = jnp.concatenate([piece, from_after, far_top, far_bottom, from_before], axis=0)
    return jnp.roll(relative, here * rows, axis=0)


def ring_scatter(whole, axis):
    count = lax.axis_size(axis)
    here = lax.axis_index(axis)
    rows = whole.shape[0] // count
    half = rows // 2
    ahead = ring_pairs(count, 1)
    behind = ring_pairs(count, -1)

    def block(offset):
        return lax.dynamic_slice_in_dim(whole, ((here + offset) % count) * rows, rows)

    far = block(2)
    sent_top = lax.ppermute(far[:half].astype(jnp.bfloat16), axis, ahead)
    sent_bottom = lax.ppermute(far[half:].astype(jnp.bfloat16), axis, behind)
    next_part = block(1)
    next_part = jnp.concatenate([next_part[:half] + sent_top.astype(jnp.float32), next_part[half:]])
    prev_part = block(-1)
    prev_part = jnp.concatenate([prev_part[:half], prev_part[half:] + sent_bottom.astype(jnp.float32)])
    got_before = lax.ppermute(next_part.astype(jnp.bfloat16), axis, ahead)
    got_after = lax.ppermute(prev_part.astype(jnp.bfloat16), axis, behind)
    return block(0) + got_before.astype(jnp.float32) + got_after.astype(jnp.float32)


def ring_pieces(piece, axis):
    count = lax.axis_size(axis)
    rows = piece.shape[0]
    half = rows // 2
    ahead = ring_pairs(count, 1)
    behind = ring_pairs(count, -1)
    from_before = lax.ppermute(piece, axis, ahead)
    from_after = lax.ppermute(piece, axis, behind)
    far_top = lax.ppermute(from_before[:half], axis, ahead)
    far_bottom = lax.ppermute(from_after[half:], axis, behind)
    return from_before, from_after, jnp.concatenate([far_top, far_bottom], axis=0)


def ring_scatter_parts(own, next_part, prev_part, far, axis):
    count = lax.axis_size(axis)
    half = own.shape[0] // 2
    ahead = ring_pairs(count, 1)
    behind = ring_pairs(count, -1)
    sent_top = lax.ppermute(far[:half].astype(jnp.bfloat16), axis, ahead)
    sent_bottom = lax.ppermute(far[half:].astype(jnp.bfloat16), axis, behind)
    next_part = jnp.concatenate([next_part[:half] + sent_top.astype(jnp.float32), next_part[half:]])
    prev_part = jnp.concatenate([prev_part[:half], prev_part[half:] + sent_bottom.astype(jnp.float32)])
    got_before = lax.ppermute(next_part.astype(jnp.bfloat16), axis, ahead)
    got_after = lax.ppermute(prev_part.astype(jnp.bfloat16), axis, behind)
    return own + got_before.astype(jnp.float32) + got_after.astype(jnp.float32)


def feed_forward(rows, widening_matrix, down_weight):
    both = jnp.einsum("rd,dtf->rtf", rows, widening_matrix, preferred_element_type=jnp.float32)
    inner = (jax.nn.silu(both[:, 0]) * both[:, 1]).astype(jnp.bfloat16)
    return jnp.dot(inner, down_weight, preferred_element_type=jnp.float32)


def rms_norm(value, gain):
    factor = lax.rsqrt(jnp.mean(value * value, axis=-1, keepdims=True) + 1e-05)
    return (value * factor * gain).astype(jnp.bfloat16)


def rope_tables(position):
    half = HD // 2
    freq = 500000.0 ** (-(jnp.arange(half).astype(jnp.float32) * 2.0 / HD))
    angle = position.astype(jnp.float32)[:, None] * freq[None, :]
    return (jnp.cos(angle), jnp.sin(angle))


def rotate(tensor, cosine, sine):
    half = tensor.shape[-1] // 2
    first = tensor[..., :half]
    second = tensor[..., half:]
    cos_part = cosine[:, None, :]
    sin_part = sine[:, None, :]
    return jnp.concatenate(
        [first * cos_part - second * sin_part, second * cos_part + first * sin_part], axis=-1
    )


def body(
    tokens,
    document_index,
    block_mask,
    slot_keys,
    mem_init,
    retain,
    attn_gain,
    mlp_gain,
    w_query,
    w_kv,
    w_out,
    w_gate_up,
    w_down,
):
    seg_local = document_index.shape[0] // SEG_LEN
    rows_all = seg_local * SEG_LEN
    cols_query = w_query.shape[2]
    local_heads = cols_query // HD
    group = HEADS // KV_HEADS
    local_kv = local_heads // group
    scale = HD ** (-0.5)
    cosine, sine = rope_tables(jnp.arange(rows_all) % SEG_LEN)
    docs = document_index.reshape(seg_local, SEG_LEN)
    causal = jnp.arange(SEG_LEN)[:, None] >= jnp.arange(SEG_LEN)[None, :]
    stream = tokens
    stored = []
    for layer in range(DEPTH_NUMBER):
        query_weight = w_query[layer]
        pair_weight = w_kv[layer]
        out_weight = w_out[layer]
        down_weight = w_down[layer]
        normed = rms_norm(stream, attn_gain[layer])
        project_piece = ring_gather(normed, "head")
        pairs = jnp.dot(
            project_piece, pair_weight, preferred_element_type=jnp.float32
        ).reshape(rows_all, local_kv, 2, HD)
        lookup_vectors = rotate(pairs[:, :, 0], cosine, sine).astype(jnp.bfloat16)
        values = pairs[:, :, 1].astype(jnp.bfloat16)
        query = rotate(
            jnp.dot(project_piece, query_weight, preferred_element_type=jnp.float32).reshape(
                rows_all, local_heads, HD
            ),
            cosine,
            sine,
        ).astype(jnp.bfloat16)
        query = query.reshape(seg_local, SEG_LEN, local_kv, group, HD)
        lookup_vectors = lookup_vectors.reshape(seg_local, SEG_LEN, local_kv, HD)
        values = values.reshape(seg_local, SEG_LEN, local_kv, HD)
        slots = slot_keys[layer].reshape(MEM, local_kv, group, HD)
        write_scores = (
            jnp.einsum(
                "mkgd,sjkd->skgmj", slots, lookup_vectors, preferred_element_type=jnp.float32
            )
            * scale
        )
        write_probs = jax.nn.softmax(write_scores, axis=-1).astype(jnp.bfloat16)
        written = jnp.einsum(
            "skgmj,sjkd->smkgd", write_probs, values, preferred_element_type=jnp.float32
        ).reshape(seg_local, MEM, cols_query)
        rates = jnp.repeat(retain[layer], HD, axis=1)[:, None, :]
        here = lax.axis_index("seg")
        count = lax.axis_size("seg")
        rate_row = rates[0]
        rate_high = rate_row.astype(jnp.bfloat16)
        rest = rate_row - rate_high.astype(jnp.float32)
        rate_mid = rest.astype(jnp.bfloat16)
        rate_low = (rest - rate_mid.astype(jnp.float32)).astype(jnp.bfloat16)
        payload = jnp.concatenate(
            [written[0].astype(jnp.bfloat16), rate_high, rate_mid, rate_low], axis=0
        )
        gathered = lax.all_gather(payload, "seg")
        written_all = gathered[:, :MEM].astype(jnp.float32)
        rate_parts = gathered[:, MEM:, ::HD].astype(jnp.float32)
        rate_all = rate_parts[:, 0] + rate_parts[:, 1] + rate_parts[:, 2]
        order = jnp.arange(count)
        inside = (order[None, :] > order[:, None]) & (order[None, :] < here)
        span = jnp.prod(jnp.where(inside[:, :, None], rate_all[None, :, :], 1.0), axis=1)
        weight = jnp.where((order < here)[:, None], span * (1.0 - rate_all), 0.0)
        carry = jnp.prod(jnp.where((order < here)[:, None], rate_all, 1.0), axis=0)
        weight = jnp.repeat(weight, HD, axis=1)
        carry = jnp.repeat(carry, HD)
        state = carry[None, :] * mem_init[layer] + jnp.sum(
            weight[:, None, :] * written_all, axis=0
        )
        if layer == 0:
            state, gate_up_slices = lax.optimization_barrier(
                (state, [w_gate_up[index] for index in range(DEPTH_NUMBER)])
            )
        segment = 0
        memory_read = state.astype(jnp.bfloat16).reshape(MEM, local_kv, group, HD)
        state = rates[segment] * state + (1.0 - rates[segment]) * written[segment]
        after_list = [state]
        blocks = jnp.repeat(jnp.repeat(block_mask[segment], BLOCK, axis=0), BLOCK, axis=1)
        allowed = causal & (docs[segment][:, None] == docs[segment][None, :]) & (blocks == 1)
        slot_scores = (
            jnp.einsum("ikgd,mkgd->kgim", query[segment], slots, preferred_element_type=jnp.float32)
            * scale
        )
        token_scores = (
            jnp.einsum(
                "ikgd,jkd->kgij",
                query[segment],
                lookup_vectors[segment],
                preferred_element_type=jnp.float32,
            )
            * scale
        )
        token_scores = jnp.where(allowed, token_scores, -jnp.inf)
        probs = jax.nn.softmax(
            jnp.concatenate([slot_scores, token_scores], axis=-1), axis=-1
        ).astype(jnp.bfloat16)
        result = jnp.einsum(
            "kgim,mkgd->ikgd", probs[..., :MEM], memory_read, preferred_element_type=jnp.float32
        )
        result = result + jnp.einsum(
            "kgij,jkd->ikgd", probs[..., MEM:], values[segment], preferred_element_type=jnp.float32
        )
        outputs = result.reshape(SEG_LEN, cols_query).astype(jnp.bfloat16)
        stored.append(jnp.stack(after_list))
        mixed = ring_scatter(
            jnp.dot(outputs, out_weight, preferred_element_type=jnp.float32), "head"
        )
        middle = stream + mixed
        mlp_piece = rms_norm(middle, mlp_gain[layer])
        from_before, from_after, far_rows = ring_pieces(mlp_piece, "head")
        widening_matrix = gate_up_slices[layer]
        own_part = feed_forward(mlp_piece, widening_matrix, down_weight)
        side_parts = feed_forward(
            jnp.concatenate([from_before, from_after], axis=0), widening_matrix, down_weight
        )
        far_part = feed_forward(far_rows, widening_matrix, down_weight)
        piece_rows = mlp_piece.shape[0]
        down = ring_scatter_parts(
            own_part, side_parts[piece_rows:], side_parts[:piece_rows], far_part, "head"
        )
        stream = middle + down
    return (stream, jnp.stack(stored))


def solution(mesh):
    return jax.shard_map(
        body,
        mesh=mesh,
        in_specs=(
            P(("seg", "head"), None),
            P("seg"),
            P("seg", None, None),
            P(None, None, "head"),
            P(None, None, "head"),
            P(None, "seg", "head"),
            P(),
            P(),
            P(None, None, "head"),
            P(None, None, "head"),
            P(None, "head", None),
            P(None, None, None, "head"),
            P(None, "head", None),
        ),
        out_specs=(P(("seg", "head"), None), P(None, "seg", None, "head")),
        check_vma=False,
    )
```

```python
import jax
import jax.numpy as jnp
from jax import lax
from jax.sharding import PartitionSpec as P

HEADS = 32
KV_HEADS = 8
HD = 64
MEM = 128
SEG_LEN = 512
BLOCK = 128
DEPTH_NUMBER = 2


def ring_pairs(count, step):
    return [(i, (i + step) % count) for i in range(count)]


def ring_gather(piece, axis):
    count = lax.axis_size(axis)
    here = lax.axis_index(axis)
    rows = piece.shape[0]
    half = rows // 2
    ahead = ring_pairs(count, 1)
    behind = ring_pairs(count, -1)
    from_before = lax.ppermute(piece, axis, ahead)
    from_after = lax.ppermute(piece, axis, behind)
    far_top = lax.ppermute(from_before[:half], axis, ahead)
    far_bottom = lax.ppermute(from_after[half:], axis, behind)
    relative = jnp.concatenate([piece, from_after, far_top, far_bottom, from_before], axis=0)
    return jnp.roll(relative, here * rows, axis=0)


def ring_scatter(whole, axis):
    count = lax.axis_size(axis)
    here = lax.axis_index(axis)
    rows = whole.shape[0] // count
    half = rows // 2
    ahead = ring_pairs(count, 1)
    behind = ring_pairs(count, -1)

    def block(offset):
        return lax.dynamic_slice_in_dim(whole, ((here + offset) % count) * rows, rows)

    far = block(2)
    sent_top = lax.ppermute(far[:half].astype(jnp.bfloat16), axis, ahead)
    sent_bottom = lax.ppermute(far[half:].astype(jnp.bfloat16), axis, behind)
    next_part = block(1)
    next_part = jnp.concatenate([next_part[:half] + sent_top.astype(jnp.float32), next_part[half:]])
    prev_part = block(-1)
    prev_part = jnp.concatenate([prev_part[:half], prev_part[half:] + sent_bottom.astype(jnp.float32)])
    got_before = lax.ppermute(next_part.astype(jnp.bfloat16), axis, ahead)
    got_after = lax.ppermute(prev_part.astype(jnp.bfloat16), axis, behind)
    return block(0) + got_before.astype(jnp.float32) + got_after.astype(jnp.float32)


def ring_pieces(piece, axis):
    count = lax.axis_size(axis)
    rows = piece.shape[0]
    half = rows // 2
    ahead = ring_pairs(count, 1)
    behind = ring_pairs(count, -1)
    from_before = lax.ppermute(piece, axis, ahead)
    from_after = lax.ppermute(piece, axis, behind)
    far_top = lax.ppermute(from_before[:half], axis, ahead)
    far_bottom = lax.ppermute(from_after[half:], axis, behind)
    return from_before, from_after, jnp.concatenate([far_top, far_bottom], axis=0)


def ring_scatter_parts(own, next_part, prev_part, far, axis):
    count = lax.axis_size(axis)
    half = own.shape[0] // 2
    ahead = ring_pairs(count, 1)
    behind = ring_pairs(count, -1)
    sent_top = lax.ppermute(far[:half].astype(jnp.bfloat16), axis, ahead)
    sent_bottom = lax.ppermute(far[half:].astype(jnp.bfloat16), axis, behind)
    next_part = jnp.concatenate([next_part[:half] + sent_top.astype(jnp.float32), next_part[half:]])
    prev_part = jnp.concatenate([prev_part[:half], prev_part[half:] + sent_bottom.astype(jnp.float32)])
    got_before = lax.ppermute(next_part.astype(jnp.bfloat16), axis, ahead)
    got_after = lax.ppermute(prev_part.astype(jnp.bfloat16), axis, behind)
    return own + got_before.astype(jnp.float32) + got_after.astype(jnp.float32)


def feed_forward(rows, widening_matrix, down_weight):
    both = jnp.einsum("rd,dtf->rtf", rows, widening_matrix, preferred_element_type=jnp.float32)
    inner = (jax.nn.silu(both[:, 0]) * both[:, 1]).astype(jnp.bfloat16)
    return jnp.dot(inner, down_weight, preferred_element_type=jnp.float32)


def rms_norm(value, gain):
    factor = lax.rsqrt(jnp.mean(value * value, axis=-1, keepdims=True) + 1e-05)
    return (value * factor * gain).astype(jnp.bfloat16)


def rope_tables(position):
    half = HD // 2
    freq = 500000.0 ** (-(jnp.arange(half).astype(jnp.float32) * 2.0 / HD))
    angle = position.astype(jnp.float32)[:, None] * freq[None, :]
    return (jnp.cos(angle), jnp.sin(angle))


def rotate(tensor, cosine, sine):
    half = tensor.shape[-1] // 2
    first = tensor[..., :half]
    second = tensor[..., half:]
    cos_part = cosine[:, None, :]
    sin_part = sine[:, None, :]
    return jnp.concatenate(
        [first * cos_part - second * sin_part, second * cos_part + first * sin_part], axis=-1
    )


def body(
    tokens,
    document_index,
    block_mask,
    slot_keys,
    mem_init,
    retain,
    attn_gain,
    mlp_gain,
    w_query,
    w_kv,
    w_out,
    w_gate_up,
    w_down,
):
    seg_local = document_index.shape[0] // SEG_LEN
    rows_all = seg_local * SEG_LEN
    cols_query = w_query.shape[2]
    local_heads = cols_query // HD
    group = HEADS // KV_HEADS
    local_kv = local_heads // group
    scale = HD ** (-0.5)
    piece_count = lax.axis_size("head")
    piece_len = SEG_LEN // piece_count
    origin = (jnp.arange(SEG_LEN) + lax.axis_index("head") * piece_len) % SEG_LEN
    cosine, sine = rope_tables(origin)
    docs = document_index.reshape(seg_local, SEG_LEN)
    causal = origin[:, None] >= origin[None, :]
    stream = tokens
    stored = []
    for layer in range(DEPTH_NUMBER):
        query_weight = w_query[layer]
        pair_weight = w_kv[layer]
        out_weight = w_out[layer]
        down_weight = w_down[layer]
        normed = rms_norm(stream, attn_gain[layer])
        from_before, from_after, far_rows = ring_pieces(normed, "head")
        project_piece = jnp.concatenate([normed, from_after, far_rows, from_before], axis=0)
        pairs = jnp.dot(
            project_piece, pair_weight, preferred_element_type=jnp.float32
        ).reshape(rows_all, local_kv, 2, HD)
        lookup_vectors = rotate(pairs[:, :, 0], cosine, sine).astype(jnp.bfloat16)
        values = pairs[:, :, 1].astype(jnp.bfloat16)
        query = rotate(
            jnp.dot(project_piece, query_weight, preferred_element_type=jnp.float32).reshape(
                rows_all, local_heads, HD
            ),
            cosine,
            sine,
        ).astype(jnp.bfloat16)
        query = query.reshape(seg_local, SEG_LEN, local_kv, group, HD)
        lookup_vectors = lookup_vectors.reshape(seg_local, SEG_LEN, local_kv, HD)
        values = values.reshape(seg_local, SEG_LEN, local_kv, HD)
        slots = slot_keys[layer].reshape(MEM, local_kv, group, HD)
        write_scores = (
            jnp.einsum(
                "mkgd,sjkd->skgmj", slots, lookup_vectors, preferred_element_type=jnp.float32
            )
            * scale
        )
        write_probs = jax.nn.softmax(write_scores, axis=-1).astype(jnp.bfloat16)
        written = jnp.einsum(
            "skgmj,sjkd->smkgd", write_probs, values, preferred_element_type=jnp.float32
        ).reshape(seg_local, MEM, cols_query)
        rates = jnp.repeat(retain[layer], HD, axis=1)[:, None, :]
        here = lax.axis_index("seg")
        count = lax.axis_size("seg")
        rate_row = rates[0]
        rate_high = rate_row.astype(jnp.bfloat16)
        rest = rate_row - rate_high.astype(jnp.float32)
        rate_mid = rest.astype(jnp.bfloat16)
        rate_low = (rest - rate_mid.astype(jnp.float32)).astype(jnp.bfloat16)
        payload = jnp.concatenate(
            [written[0].astype(jnp.bfloat16), rate_high, rate_mid, rate_low], axis=0
        )
        gathered = lax.all_gather(payload, "seg")
        written_all = gathered[:, :MEM].astype(jnp.float32)
        rate_parts = gathered[:, MEM:, ::HD].astype(jnp.float32)
        rate_all = rate_parts[:, 0] + rate_parts[:, 1] + rate_parts[:, 2]
        order = jnp.arange(count)
        inside = (order[None, :] > order[:, None]) & (order[None, :] < here)
        span = jnp.prod(jnp.where(inside[:, :, None], rate_all[None, :, :], 1.0), axis=1)
        weight = jnp.where((order < here)[:, None], span * (1.0 - rate_all), 0.0)
        carry = jnp.prod(jnp.where((order < here)[:, None], rate_all, 1.0), axis=0)
        weight = jnp.repeat(weight, HD, axis=1)
        carry = jnp.repeat(carry, HD)
        state = carry[None, :] * mem_init[layer] + jnp.sum(
            weight[:, None, :] * written_all, axis=0
        )
        if layer == 0:
            state, gate_up_slices = lax.optimization_barrier(
                (state, [w_gate_up[index] for index in range(DEPTH_NUMBER)])
            )
        segment = 0
        memory_read = state.astype(jnp.bfloat16).reshape(MEM, local_kv, group, HD)
        state = rates[segment] * state + (1.0 - rates[segment]) * written[segment]
        after_list = [state]
        block_of = origin // BLOCK
        blocks = block_mask[segment][block_of[:, None], block_of[None, :]]
        seg_docs = docs[segment][origin]
        allowed = causal & (seg_docs[:, None] == seg_docs[None, :]) & (blocks == 1)
        slot_scores = (
            jnp.einsum("ikgd,mkgd->kgim", query[segment], slots, preferred_element_type=jnp.float32)
            * scale
        )
        token_scores = (
            jnp.einsum(
                "ikgd,jkd->kgij",
                query[segment],
                lookup_vectors[segment],
                preferred_element_type=jnp.float32,
            )
            * scale
        )
        token_scores = jnp.where(allowed, token_scores, -jnp.inf)
        probs = jax.nn.softmax(
            jnp.concatenate([slot_scores, token_scores], axis=-1), axis=-1
        ).astype(jnp.bfloat16)
        result = jnp.einsum(
            "kgim,mkgd->ikgd", probs[..., :MEM], memory_read, preferred_element_type=jnp.float32
        )
        result = result + jnp.einsum(
            "kgij,jkd->ikgd", probs[..., MEM:], values[segment], preferred_element_type=jnp.float32
        )
        outputs = result.reshape(SEG_LEN, cols_query).astype(jnp.bfloat16)
        stored.append(jnp.stack(after_list))
        mixed_parts = jnp.dot(outputs, out_weight, preferred_element_type=jnp.float32)
        mixed = ring_scatter_parts(
            mixed_parts[:piece_len],
            mixed_parts[piece_len : 2 * piece_len],
            mixed_parts[3 * piece_len :],
            mixed_parts[2 * piece_len : 3 * piece_len],
            "head",
        )
        middle = stream + mixed
        mlp_piece = rms_norm(middle, mlp_gain[layer])
        from_before, from_after, far_rows = ring_pieces(mlp_piece, "head")
        widening_matrix = gate_up_slices[layer]
        own_part = feed_forward(mlp_piece, widening_matrix, down_weight)
        side_parts = feed_forward(
            jnp.concatenate([from_before, from_after], axis=0), widening_matrix, down_weight
        )
        far_part = feed_forward(far_rows, widening_matrix, down_weight)
        piece_rows = mlp_piece.shape[0]
        down = ring_scatter_parts(
            own_part, side_parts[piece_rows:], side_parts[:piece_rows], far_part, "head"
        )
        stream = middle + down
    return (stream, jnp.stack(stored))


def solution(mesh):
    return jax.shard_map(
        body,
        mesh=mesh,
        in_specs=(
            P(("seg", "head"), None),
            P("seg"),
            P("seg", None, None),
            P(None, None, "head"),
            P(None, None, "head"),
            P(None, "seg", "head"),
            P(),
            P(),
            P(None, None, "head"),
            P(None, None, "head"),
            P(None, "head", None),
            P(None, None, None, "head"),
            P(None, "head", None),
        ),
        out_specs=(P(("seg", "head"), None), P(None, "seg", None, "head")),
        check_vma=False,
    )
```

```python
import jax
import jax.numpy as jnp
from jax import lax
from jax.sharding import PartitionSpec as P

HEADS = 32
KV_HEADS = 8
HD = 64
MEM = 128
SEG_LEN = 512
BLOCK = 128
DEPTH_NUMBER = 2


def ring_pairs(count, step):
    return [(i, (i + step) % count) for i in range(count)]


def ring_gather(piece, axis):
    count = lax.axis_size(axis)
    here = lax.axis_index(axis)
    rows = piece.shape[0]
    half = rows // 2
    ahead = ring_pairs(count, 1)
    behind = ring_pairs(count, -1)
    from_before = lax.ppermute(piece, axis, ahead)
    from_after = lax.ppermute(piece, axis, behind)
    far_top = lax.ppermute(from_before[:half], axis, ahead)
    far_bottom = lax.ppermute(from_after[half:], axis, behind)
    relative = jnp.concatenate([piece, from_after, far_top, far_bottom, from_before], axis=0)
    return jnp.roll(relative, here * rows, axis=0)


def ring_scatter(whole, axis):
    count = lax.axis_size(axis)
    here = lax.axis_index(axis)
    rows = whole.shape[0] // count
    half = rows // 2
    ahead = ring_pairs(count, 1)
    behind = ring_pairs(count, -1)

    def block(offset):
        return lax.dynamic_slice_in_dim(whole, ((here + offset) % count) * rows, rows)

    far = block(2)
    sent_top = lax.ppermute(far[:half].astype(jnp.bfloat16), axis, ahead)
    sent_bottom = lax.ppermute(far[half:].astype(jnp.bfloat16), axis, behind)
    next_part = block(1)
    next_part = jnp.concatenate([next_part[:half] + sent_top.astype(jnp.float32), next_part[half:]])
    prev_part = block(-1)
    prev_part = jnp.concatenate([prev_part[:half], prev_part[half:] + sent_bottom.astype(jnp.float32)])
    got_before = lax.ppermute(next_part.astype(jnp.bfloat16), axis, ahead)
    got_after = lax.ppermute(prev_part.astype(jnp.bfloat16), axis, behind)
    return block(0) + got_before.astype(jnp.float32) + got_after.astype(jnp.float32)


def ring_pieces(piece, axis):
    count = lax.axis_size(axis)
    rows = piece.shape[0]
    half = rows // 2
    ahead = ring_pairs(count, 1)
    behind = ring_pairs(count, -1)
    from_before = lax.ppermute(piece, axis, ahead)
    from_after = lax.ppermute(piece, axis, behind)
    far_top = lax.ppermute(from_before[:half], axis, ahead)
    far_bottom = lax.ppermute(from_after[half:], axis, behind)
    return from_before, from_after, jnp.concatenate([far_top, far_bottom], axis=0)


def ring_scatter_parts(own, next_part, prev_part, far, axis):
    count = lax.axis_size(axis)
    half = own.shape[0] // 2
    ahead = ring_pairs(count, 1)
    behind = ring_pairs(count, -1)
    sent_top = lax.ppermute(far[:half].astype(jnp.bfloat16), axis, ahead)
    sent_bottom = lax.ppermute(far[half:].astype(jnp.bfloat16), axis, behind)
    next_part = jnp.concatenate([next_part[:half] + sent_top.astype(jnp.float32), next_part[half:]])
    prev_part = jnp.concatenate([prev_part[:half], prev_part[half:] + sent_bottom.astype(jnp.float32)])
    got_before = lax.ppermute(next_part.astype(jnp.bfloat16), axis, ahead)
    got_after = lax.ppermute(prev_part.astype(jnp.bfloat16), axis, behind)
    return own + got_before.astype(jnp.float32) + got_after.astype(jnp.float32)


def feed_forward(rows, widening_matrix, down_weight):
    both = jnp.einsum("rd,dtf->rtf", rows, widening_matrix, preferred_element_type=jnp.float32)
    inner = (jax.nn.silu(both[:, 0]) * both[:, 1]).astype(jnp.bfloat16)
    return jnp.dot(inner, down_weight, preferred_element_type=jnp.float32)


def rms_norm(value, gain):
    factor = lax.rsqrt(jnp.mean(value * value, axis=-1, keepdims=True) + 1e-05)
    return (value * factor * gain).astype(jnp.bfloat16)


def rope_tables(position):
    half = HD // 2
    freq = 500000.0 ** (-(jnp.arange(half).astype(jnp.float32) * 2.0 / HD))
    angle = position.astype(jnp.float32)[:, None] * freq[None, :]
    return (jnp.cos(angle), jnp.sin(angle))


def rotate(tensor, cosine, sine):
    half = tensor.shape[-1] // 2
    first = tensor[..., :half]
    second = tensor[..., half:]
    cos_part = cosine[:, None, :]
    sin_part = sine[:, None, :]
    return jnp.concatenate(
        [first * cos_part - second * sin_part, second * cos_part + first * sin_part], axis=-1
    )


def body(
    tokens,
    document_index,
    block_mask,
    slot_keys,
    mem_init,
    retain,
    attn_gain,
    mlp_gain,
    w_query,
    w_kv,
    w_out,
    w_gate_up,
    w_down,
):
    seg_local = document_index.shape[0] // SEG_LEN
    rows_all = seg_local * SEG_LEN
    cols_query = w_query.shape[2]
    local_heads = cols_query // HD
    group = HEADS // KV_HEADS
    local_kv = local_heads // group
    scale = HD ** (-0.5)
    piece_count = lax.axis_size("head")
    piece_len = SEG_LEN // piece_count
    origin = (jnp.arange(SEG_LEN) + lax.axis_index("head") * piece_len) % SEG_LEN
    cosine, sine = rope_tables(origin)
    docs = document_index.reshape(seg_local, SEG_LEN)
    causal = origin[:, None] >= origin[None, :]
    stream = tokens
    stored = []
    for layer in range(DEPTH_NUMBER):
        query_weight = w_query[layer]
        pair_weight = w_kv[layer]
        out_weight = w_out[layer]
        down_weight = w_down[layer]
        normed = rms_norm(stream, attn_gain[layer])
        from_before, from_after, far_rows = ring_pieces(normed, "head")
        project_piece = jnp.concatenate([normed, from_after, far_rows, from_before], axis=0)
        pairs = jnp.dot(
            project_piece, pair_weight, preferred_element_type=jnp.float32
        ).reshape(rows_all, local_kv, 2, HD)
        lookup_vectors = rotate(pairs[:, :, 0], cosine, sine).astype(jnp.bfloat16)
        values = pairs[:, :, 1].astype(jnp.bfloat16)
        query = rotate(
            jnp.dot(project_piece, query_weight, preferred_element_type=jnp.float32).reshape(
                rows_all, local_heads, HD
            ),
            cosine,
            sine,
        ).astype(jnp.bfloat16)
        query = query.reshape(seg_local, SEG_LEN, local_kv, group, HD)
        lookup_vectors = lookup_vectors.reshape(seg_local, SEG_LEN, local_kv, HD)
        values = values.reshape(seg_local, SEG_LEN, local_kv, HD)
        slots = slot_keys[layer].reshape(MEM, local_kv, group, HD)
        write_scores = (
            jnp.einsum(
                "mkgd,sjkd->skgmj", slots, lookup_vectors, preferred_element_type=jnp.float32
            )
            * scale
        )
        write_probs = jax.nn.softmax(write_scores, axis=-1).astype(jnp.bfloat16)
        written = jnp.einsum(
            "skgmj,sjkd->smkgd", write_probs, values, preferred_element_type=jnp.float32
        ).reshape(seg_local, MEM, cols_query)
        rates = jnp.repeat(retain[layer], HD, axis=1)[:, None, :]
        here = lax.axis_index("seg")
        count = lax.axis_size("seg")
        rate_row = rates[0]
        rate_high = rate_row.astype(jnp.bfloat16)
        rest = rate_row - rate_high.astype(jnp.float32)
        rate_mid = rest.astype(jnp.bfloat16)
        rate_low = (rest - rate_mid.astype(jnp.float32)).astype(jnp.bfloat16)
        payload = jnp.concatenate(
            [written[0].astype(jnp.bfloat16), rate_high, rate_mid, rate_low], axis=0
        )
        gathered = lax.all_gather(payload, "seg")
        written_all = gathered[:, :MEM].astype(jnp.float32)
        rate_parts = gathered[:, MEM:, ::HD].astype(jnp.float32)
        rate_all = rate_parts[:, 0] + rate_parts[:, 1] + rate_parts[:, 2]
        order = jnp.arange(count)
        inside = (order[None, :] > order[:, None]) & (order[None, :] < here)
        span = jnp.prod(jnp.where(inside[:, :, None], rate_all[None, :, :], 1.0), axis=1)
        weight = jnp.where((order < here)[:, None], span * (1.0 - rate_all), 0.0)
        carry = jnp.prod(jnp.where((order < here)[:, None], rate_all, 1.0), axis=0)
        weight = jnp.repeat(weight, HD, axis=1)
        carry = jnp.repeat(carry, HD)
        state = carry[None, :] * mem_init[layer] + jnp.sum(
            weight[:, None, :] * written_all, axis=0
        )
        if layer == 0:
            state, gate_up_slices = lax.optimization_barrier(
                (state, [w_gate_up[index] for index in range(DEPTH_NUMBER)])
            )
        segment = 0
        memory_read = state.astype(jnp.bfloat16).reshape(MEM, local_kv, group, HD)
        state = rates[segment] * state + (1.0 - rates[segment]) * written[segment]
        after_list = [state]
        shift = -lax.axis_index("head") * piece_len
        blocks = jnp.repeat(jnp.repeat(block_mask[segment], BLOCK, axis=0), BLOCK, axis=1)
        blocks = jnp.roll(jnp.roll(blocks, shift, axis=0), shift, axis=1)
        seg_docs = jnp.roll(docs[segment], shift)
        allowed = causal & (seg_docs[:, None] == seg_docs[None, :]) & (blocks == 1)
        slot_scores = (
            jnp.einsum("ikgd,mkgd->kgim", query[segment], slots, preferred_element_type=jnp.float32)
            * scale
        )
        token_scores = (
            jnp.einsum(
                "ikgd,jkd->kgij",
                query[segment],
                lookup_vectors[segment],
                preferred_element_type=jnp.float32,
            )
            * scale
        )
        token_scores = jnp.where(allowed, token_scores, -jnp.inf)
        probs = jax.nn.softmax(
            jnp.concatenate([slot_scores, token_scores], axis=-1), axis=-1
        ).astype(jnp.bfloat16)
        result = jnp.einsum(
            "kgim,mkgd->ikgd", probs[..., :MEM], memory_read, preferred_element_type=jnp.float32
        )
        result = result + jnp.einsum(
            "kgij,jkd->ikgd", probs[..., MEM:], values[segment], preferred_element_type=jnp.float32
        )
        outputs = result.reshape(SEG_LEN, cols_query).astype(jnp.bfloat16)
        stored.append(jnp.stack(after_list))
        mixed_parts = jnp.dot(outputs, out_weight, preferred_element_type=jnp.float32)
        mixed = ring_scatter_parts(
            mixed_parts[:piece_len],
            mixed_parts[piece_len : 2 * piece_len],
            mixed_parts[3 * piece_len :],
            mixed_parts[2 * piece_len : 3 * piece_len],
            "head",
        )
        middle = stream + mixed
        mlp_piece = rms_norm(middle, mlp_gain[layer])
        from_before, from_after, far_rows = ring_pieces(mlp_piece, "head")
        widening_matrix = gate_up_slices[layer]
        own_part = feed_forward(mlp_piece, widening_matrix, down_weight)
        side_parts = feed_forward(
            jnp.concatenate([from_before, from_after], axis=0), widening_matrix, down_weight
        )
        far_part = feed_forward(far_rows, widening_matrix, down_weight)
        piece_rows = mlp_piece.shape[0]
        down = ring_scatter_parts(
            own_part, side_parts[piece_rows:], side_parts[:piece_rows], far_part, "head"
        )
        stream = middle + down
    return (stream, jnp.stack(stored))


def solution(mesh):
    return jax.shard_map(
        body,
        mesh=mesh,
        in_specs=(
            P(("seg", "head"), None),
            P("seg"),
            P("seg", None, None),
            P(None, None, "head"),
            P(None, None, "head"),
            P(None, "seg", "head"),
            P(),
            P(),
            P(None, None, "head"),
            P(None, None, "head"),
            P(None, "head", None),
            P(None, None, None, "head"),
            P(None, "head", None),
        ),
        out_specs=(P(("seg", "head"), None), P(None, "seg", None, "head")),
        check_vma=False,
    )
```

```python
import jax
import jax.numpy as jnp
from jax import lax
from jax.sharding import PartitionSpec as P

HEADS = 32
KV_HEADS = 8
HD = 64
MEM = 128
SEG_LEN = 512
BLOCK = 128
DEPTH_NUMBER = 2


def ring_pairs(count, step):
    return [(i, (i + step) % count) for i in range(count)]


def ring_gather(piece, axis):
    count = lax.axis_size(axis)
    here = lax.axis_index(axis)
    rows = piece.shape[0]
    half = rows // 2
    ahead = ring_pairs(count, 1)
    behind = ring_pairs(count, -1)
    from_before = lax.ppermute(piece, axis, ahead)
    from_after = lax.ppermute(piece, axis, behind)
    far_top = lax.ppermute(from_before[:half], axis, ahead)
    far_bottom = lax.ppermute(from_after[half:], axis, behind)
    relative = jnp.concatenate([piece, from_after, far_top, far_bottom, from_before], axis=0)
    return jnp.roll(relative, here * rows, axis=0)


def ring_scatter(whole, axis):
    count = lax.axis_size(axis)
    here = lax.axis_index(axis)
    rows = whole.shape[0] // count
    half = rows // 2
    ahead = ring_pairs(count, 1)
    behind = ring_pairs(count, -1)

    def block(offset):
        return lax.dynamic_slice_in_dim(whole, ((here + offset) % count) * rows, rows)

    far = block(2)
    sent_top = lax.ppermute(far[:half].astype(jnp.bfloat16), axis, ahead)
    sent_bottom = lax.ppermute(far[half:].astype(jnp.bfloat16), axis, behind)
    next_part = block(1)
    next_part = jnp.concatenate([next_part[:half] + sent_top.astype(jnp.float32), next_part[half:]])
    prev_part = block(-1)
    prev_part = jnp.concatenate([prev_part[:half], prev_part[half:] + sent_bottom.astype(jnp.float32)])
    got_before = lax.ppermute(next_part.astype(jnp.bfloat16), axis, ahead)
    got_after = lax.ppermute(prev_part.astype(jnp.bfloat16), axis, behind)
    return block(0) + got_before.astype(jnp.float32) + got_after.astype(jnp.float32)


def ring_pieces(piece, axis):
    count = lax.axis_size(axis)
    rows = piece.shape[0]
    half = rows // 2
    ahead = ring_pairs(count, 1)
    behind = ring_pairs(count, -1)
    from_before = lax.ppermute(piece, axis, ahead)
    from_after = lax.ppermute(piece, axis, behind)
    far_top = lax.ppermute(from_before[:half], axis, ahead)
    far_bottom = lax.ppermute(from_after[half:], axis, behind)
    return from_before, from_after, jnp.concatenate([far_top, far_bottom], axis=0)


def ring_scatter_parts(own, next_part, prev_part, far, axis):
    count = lax.axis_size(axis)
    half = own.shape[0] // 2
    ahead = ring_pairs(count, 1)
    behind = ring_pairs(count, -1)
    sent_top = lax.ppermute(far[:half].astype(jnp.bfloat16), axis, ahead)
    sent_bottom = lax.ppermute(far[half:].astype(jnp.bfloat16), axis, behind)
    next_part = jnp.concatenate([next_part[:half] + sent_top.astype(jnp.float32), next_part[half:]])
    prev_part = jnp.concatenate([prev_part[:half], prev_part[half:] + sent_bottom.astype(jnp.float32)])
    got_before = lax.ppermute(next_part.astype(jnp.bfloat16), axis, ahead)
    got_after = lax.ppermute(prev_part.astype(jnp.bfloat16), axis, behind)
    return own + got_before.astype(jnp.float32) + got_after.astype(jnp.float32)


def feed_forward(rows, widening_matrix, down_weight):
    both = jnp.einsum("rd,dtf->rtf", rows, widening_matrix, preferred_element_type=jnp.float32)
    inner = (jax.nn.silu(both[:, 0]) * both[:, 1]).astype(jnp.bfloat16)
    return jnp.dot(inner, down_weight, preferred_element_type=jnp.float32)


def rms_norm(value, gain):
    factor = lax.rsqrt(jnp.mean(value * value, axis=-1, keepdims=True) + 1e-05)
    return (value * factor * gain).astype(jnp.bfloat16)


def rope_tables(position):
    half = HD // 2
    freq = 500000.0 ** (-(jnp.arange(half).astype(jnp.float32) * 2.0 / HD))
    angle = position.astype(jnp.float32)[:, None] * freq[None, :]
    return (jnp.cos(angle), jnp.sin(angle))


def rotate(tensor, cosine, sine):
    half = tensor.shape[-1] // 2
    first = tensor[..., :half]
    second = tensor[..., half:]
    cos_part = cosine[:, None, :]
    sin_part = sine[:, None, :]
    return jnp.concatenate(
        [first * cos_part - second * sin_part, second * cos_part + first * sin_part], axis=-1
    )


def body(
    tokens,
    document_index,
    block_mask,
    slot_keys,
    mem_init,
    retain,
    attn_gain,
    mlp_gain,
    w_query,
    w_kv,
    w_out,
    w_gate_up,
    w_down,
):
    seg_local = document_index.shape[0] // SEG_LEN
    rows_all = seg_local * SEG_LEN
    cols_query = w_query.shape[2]
    local_heads = cols_query // HD
    group = HEADS // KV_HEADS
    local_kv = local_heads // group
    scale = HD ** (-0.5)
    piece_count = lax.axis_size("head")
    piece_len = SEG_LEN // piece_count
    origin = (jnp.arange(SEG_LEN) + lax.axis_index("head") * piece_len) % SEG_LEN
    cosine, sine = rope_tables(origin)
    docs = document_index.reshape(seg_local, SEG_LEN)
    causal = origin[:, None] >= origin[None, :]
    stream = tokens
    stored = []
    for layer in range(DEPTH_NUMBER):
        query_weight = w_query[layer]
        pair_weight = w_kv[layer]
        out_weight = w_out[layer]
        down_weight = w_down[layer]
        normed = rms_norm(stream, attn_gain[layer])
        from_before, from_after, far_rows = ring_pieces(normed, "head")
        project_piece = jnp.concatenate([normed, from_after, far_rows, from_before], axis=0)
        pairs = jnp.concatenate(
            [
                jnp.dot(normed, pair_weight, preferred_element_type=jnp.float32),
                jnp.dot(
                    jnp.concatenate([from_after, far_rows, from_before], axis=0),
                    pair_weight,
                    preferred_element_type=jnp.float32,
                ),
            ],
            axis=0,
        ).reshape(rows_all, local_kv, 2, HD)
        lookup_vectors = rotate(pairs[:, :, 0], cosine, sine).astype(jnp.bfloat16)
        values = pairs[:, :, 1].astype(jnp.bfloat16)
        query = rotate(
            jnp.dot(project_piece, query_weight, preferred_element_type=jnp.float32).reshape(
                rows_all, local_heads, HD
            ),
            cosine,
            sine,
        ).astype(jnp.bfloat16)
        query = query.reshape(seg_local, SEG_LEN, local_kv, group, HD)
        lookup_vectors = lookup_vectors.reshape(seg_local, SEG_LEN, local_kv, HD)
        values = values.reshape(seg_local, SEG_LEN, local_kv, HD)
        slots = slot_keys[layer].reshape(MEM, local_kv, group, HD)
        write_scores = (
            jnp.einsum(
                "mkgd,sjkd->skgmj", slots, lookup_vectors, preferred_element_type=jnp.float32
            )
            * scale
        )
        write_probs = jax.nn.softmax(write_scores, axis=-1).astype(jnp.bfloat16)
        written = jnp.einsum(
            "skgmj,sjkd->smkgd", write_probs, values, preferred_element_type=jnp.float32
        ).reshape(seg_local, MEM, cols_query)
        rates = jnp.repeat(retain[layer], HD, axis=1)[:, None, :]
        here = lax.axis_index("seg")
        count = lax.axis_size("seg")
        rate_row = rates[0]
        rate_high = rate_row.astype(jnp.bfloat16)
        rest = rate_row - rate_high.astype(jnp.float32)
        rate_mid = rest.astype(jnp.bfloat16)
        rate_low = (rest - rate_mid.astype(jnp.float32)).astype(jnp.bfloat16)
        payload = jnp.concatenate(
            [written[0].astype(jnp.bfloat16), rate_high, rate_mid, rate_low], axis=0
        )
        gathered = lax.all_gather(payload, "seg")
        written_all = gathered[:, :MEM].astype(jnp.float32)
        rate_parts = gathered[:, MEM:, ::HD].astype(jnp.float32)
        rate_all = rate_parts[:, 0] + rate_parts[:, 1] + rate_parts[:, 2]
        order = jnp.arange(count)
        inside = (order[None, :] > order[:, None]) & (order[None, :] < here)
        span = jnp.prod(jnp.where(inside[:, :, None], rate_all[None, :, :], 1.0), axis=1)
        weight = jnp.where((order < here)[:, None], span * (1.0 - rate_all), 0.0)
        carry = jnp.prod(jnp.where((order < here)[:, None], rate_all, 1.0), axis=0)
        weight = jnp.repeat(weight, HD, axis=1)
        carry = jnp.repeat(carry, HD)
        state = carry[None, :] * mem_init[layer] + jnp.sum(
            weight[:, None, :] * written_all, axis=0
        )
        if layer == 0:
            state, gate_up_slices = lax.optimization_barrier(
                (state, [w_gate_up[index] for index in range(DEPTH_NUMBER)])
            )
        segment = 0
        memory_read = state.astype(jnp.bfloat16).reshape(MEM, local_kv, group, HD)
        state = rates[segment] * state + (1.0 - rates[segment]) * written[segment]
        after_list = [state]
        shift = -lax.axis_index("head") * piece_len
        blocks = jnp.repeat(jnp.repeat(block_mask[segment], BLOCK, axis=0), BLOCK, axis=1)
        blocks = jnp.roll(jnp.roll(blocks, shift, axis=0), shift, axis=1)
        seg_docs = jnp.roll(docs[segment], shift)
        allowed = causal & (seg_docs[:, None] == seg_docs[None, :]) & (blocks == 1)
        slot_scores = (
            jnp.einsum("ikgd,mkgd->kgim", query[segment], slots, preferred_element_type=jnp.float32)
            * scale
        )
        token_scores = (
            jnp.einsum(
                "ikgd,jkd->kgij",
                query[segment],
                lookup_vectors[segment],
                preferred_element_type=jnp.float32,
            )
            * scale
        )
        token_scores = jnp.where(allowed, token_scores, -jnp.inf)
        probs = jax.nn.softmax(
            jnp.concatenate([slot_scores, token_scores], axis=-1), axis=-1
        ).astype(jnp.bfloat16)
        result = jnp.einsum(
            "kgim,mkgd->ikgd", probs[..., :MEM], memory_read, preferred_element_type=jnp.float32
        )
        result = result + jnp.einsum(
            "kgij,jkd->ikgd", probs[..., MEM:], values[segment], preferred_element_type=jnp.float32
        )
        outputs = result.reshape(SEG_LEN, cols_query).astype(jnp.bfloat16)
        stored.append(jnp.stack(after_list))
        mixed_parts = jnp.dot(outputs, out_weight, preferred_element_type=jnp.float32)
        mixed = ring_scatter_parts(
            mixed_parts[:piece_len],
            mixed_parts[piece_len : 2 * piece_len],
            mixed_parts[3 * piece_len :],
            mixed_parts[2 * piece_len : 3 * piece_len],
            "head",
        )
        middle = stream + mixed
        mlp_piece = rms_norm(middle, mlp_gain[layer])
        from_before, from_after, far_rows = ring_pieces(mlp_piece, "head")
        widening_matrix = gate_up_slices[layer]
        own_part = feed_forward(mlp_piece, widening_matrix, down_weight)
        side_parts = feed_forward(
            jnp.concatenate([from_before, from_after], axis=0), widening_matrix, down_weight
        )
        far_part = feed_forward(far_rows, widening_matrix, down_weight)
        piece_rows = mlp_piece.shape[0]
        down = ring_scatter_parts(
            own_part, side_parts[piece_rows:], side_parts[:piece_rows], far_part, "head"
        )
        stream = middle + down
    return (stream, jnp.stack(stored))


def solution(mesh):
    return jax.shard_map(
        body,
        mesh=mesh,
        in_specs=(
            P(("seg", "head"), None),
            P("seg"),
            P("seg", None, None),
            P(None, None, "head"),
            P(None, None, "head"),
            P(None, "seg", "head"),
            P(),
            P(),
            P(None, None, "head"),
            P(None, None, "head"),
            P(None, "head", None),
            P(None, None, None, "head"),
            P(None, "head", None),
        ),
        out_specs=(P(("seg", "head"), None), P(None, "seg", None, "head")),
        check_vma=False,
    )
```
